128 devices in a mesh: pb: 8 (over z, core), pa: 16 (over y, x).
Axes of the slice: x: 4, y: 4, z: 4, core: 2. Of those that a mesh axis runs over, the one named last changes fastest.
Arguments:
- query_states: bfloat16 [512, 32, 768], P(('pb', 'pa')), may hold values from -6 to 6
- passage_states: bfloat16 [4096, 180, 768], P(('pb', 'pa')), may hold values from -6 to 6
- head: bfloat16 [768, 128], replicated, may hold values from -0.21875 to 0.21875
- teacher: float32 [512, 32], P(('pb', 'pa')), may hold values from -8 to 8
- cand_owner: int32 [512, 32], P(('pb', 'pa')), may hold values from 0 to 127, all different within a row; in each aligned block of 4 rows (0 to 3, 4 to 7, ...) at most 2 rows name the same one
- cand_local: int32 [512, 32], P(('pb', 'pa')), may hold values from 0 to 31
- query_lengths: int32 [512], P(('pb', 'pa')), may hold values from 1 to 32, 12288 in all
- passage_lengths: int32 [4096], P(('pb', 'pa')), may hold values from 1 to 180, 491520 in all
Outputs:
- scores: float32 [512, 32], P(('pb', 'pa'))
- loss: float32 [], replicated
- head_grad: float32 [768, 128], replicated
The draws below stay inside these ranges and needn't reach their ends.
Inputs may be any that keep to these rules, and one draw needn't show every extreme that they name: `cand_owner`: each row names 32 different devices; among the rows of one device no device is named by more than 2 rows.
All inputs are finite; a program needn't handle non-finite values. No bound on the sum of `query_lengths` or of `passage_lengths` on one device may be relied on, other than what follows from the above.
Results may differ from the reference program's by a relative error of at most 0.0078.
Values may be sent and summed in bfloat16 or wider, within the bound.
No kernel may reach another device: no remote copies, remote signals or barrier semaphores. Data moves between devices by JAX's collectives and lax.ppermute only.
A program may use at most 192 MiB of HBM per device.

```python
import math
import jax
import jax.numpy as jnp
import numpy as np
from jax import lax

H = 768
D = 128
QLEN = 32
PLEN = 180
K = 32
QDEV = 4
PDEV = 32
NQ = 512
NP = 4096
CAP = 2
DEVICES = 128


def with_ends(result, stream_key, least, largest):
    longest = result.shape.index(max(result.shape))
    spots = []
    for shift in (0, 1):
        where = [jax.random.randint(jax.random.fold_in(stream_key, axis), (), 0, length) for axis, length in enumerate(result.shape)]
        where[longest] = (where[longest] + shift) % result.shape[longest]
        spots.append(tuple(where))
    return result.at[spots[0]].set(least).at[spots[1]].set(largest)


def levels(stream_key, extent, shards, least, high):
    def one(position, parts):
        steps = jax.random.uniform(jax.random.fold_in(jax.random.fold_in(stream_key, 6), position), (parts,), jnp.float32, least / len(shards), high / len(shards))
        return jnp.repeat(jnp.exp(steps), extent[position] // parts).reshape((-1,) + (1,) * (len(extent) - position - 1))

    factor_of = one(*shards[0])
    for cut in shards[1:]:
        factor_of = factor_of * one(*cut)
    return factor_of


def length_profile(amount, total, reach, lean):
    loads = [(1 << 20) // math.isqrt(grade ** lean) + 1 for grade in range(2, amount + 1)]
    surplus, holding = total - reach - (amount - 1), [1] * (amount - 1)
    while surplus > 0:
        movable = [i for i in range(amount - 1) if holding[i] < reach]
        whole, left = sum([loads[i] for i in movable]), surplus
        for i in movable:
            more = min(reach - holding[i], max(1, left * loads[i] // whole), surplus)
            holding[i] = holding[i] + more
            surplus = surplus - more
    return np.array([reach] + holding)


def uneven_parts(key, count, total, most, slope):
    if count == 2:
        one = jax.random.randint(key, (), max(1, total - most), min(most, total - 1) + 1)
        return jnp.stack([one, total - one])
    lengths = jnp.asarray(length_profile(count, total, most, slope), jnp.int32)
    twos = (count - 1) // 2
    donor, receiver = lengths[1:1 + 2 * twos:2], lengths[2:2 + 2 * twos:2]
    slack = jnp.minimum(donor - 1, most - receiver)
    passed = jax.random.randint(jax.random.fold_in(key, 1), (twos,), 0, 1 << 20) % (slack + 1)
    lengths = lengths.at[1:1 + 2 * twos:2].set(donor - passed).at[2:2 + 2 * twos:2].set(receiver + passed)
    return lengths[jax.random.permutation(jax.random.fold_in(key, 2), count)]


def shared_out(own_key, own, number, rows, count, top, limit, skew):
    order = jax.random.permutation(own_key, count)
    heavy_load, usual = shares(count, rows * top, limit, skew, True), shares(count, rows * top, limit, skew, False)
    places = jnp.arange(count)

    def named(lengths, turn):
        used = int((lengths > 0).sum())
        fixed = max(1, used // 4)
        moved = fixed + (places - fixed + turn * (used - fixed)) % max(1, count - fixed)
        return jnp.zeros((count,), jnp.int32).at[order[jnp.where(places < fixed, places, moved)]].set(jnp.asarray(lengths, jnp.int32))

    lengths = jnp.where(number % 4 == 0, named(heavy_load, number // 4), named(usual, number - number // 4 - 1))
    mixed = jax.random.permutation(jax.random.fold_in(own, 3), count)
    donor, sink = mixed[0:count // 2 * 2:2], mixed[1:count // 2 * 2:2]
    margin = jnp.minimum(lengths[donor] - 1, limit - lengths[sink]) // 2
    margin = jnp.where((donor == order[0]) | (sink == order[0]) | (lengths[sink] == 0), 0, jnp.maximum(margin, 0))
    moved = jax.random.randint(jax.random.fold_in(own, 4), (count // 2,), 0, 1 << 20) % (margin + 1)
    lengths = lengths.at[donor].add(-moved).at[sink].add(moved)
    members = jnp.searchsorted(jnp.cumsum(lengths), jnp.arange(rows * top), side="right").astype(jnp.int32)
    table = members.reshape(top, rows).T
    table = table[jax.random.permutation(jax.random.fold_in(own, 1), rows)]
    turn = jax.random.randint(jax.random.fold_in(own, 2), (rows, 1), 0, top)
    return jnp.take_along_axis(table, (jnp.arange(top)[None, :] + turn) % top, axis=1)


def shares(amount, total, limit, lean, full):
    weights = [(1 << 20) // math.isqrt(standing ** lean) + 1 for standing in range(1, amount + 1)]
    largest = limit if full else min(limit, max(-(-total // amount), total * weights[0] // sum(weights)))
    least = 1 if total - largest >= amount - 1 else 0
    counts, spare = [largest] + [least] * (amount - 1), total - largest - least * (amount - 1)
    while spare > 0:
        candidates = [i for i in range(1, amount) if counts[i] < largest] or [i for i in range(1, amount) if counts[i] < limit]
        whole, budget = sum([weights[i] for i in candidates]), spare
        for i in candidates:
            more = min(limit - counts[i], max(1, budget * weights[i] // whole), spare)
            counts[i] = counts[i] + more
            spare = spare - more
    return np.array(counts)


def centred(key, extent, deviation, reach, split=(), kind=jnp.bfloat16):
    level = levels(key, extent, split, -0.22, 0.18) if split else 1.0
    values = jax.random.normal(key, extent, jnp.float32) * deviation * level
    return jnp.minimum(jnp.maximum(values, -reach), reach).astype(kind)


def setup_inputs(seed: int = 0) -> dict:
    key_of = jax.random.split(jax.random.key(seed), 9)
    query_states = centred(key_of[0], (NQ, QLEN, H), 1.0, 6.0, ((0, 128),))
    passage_states = centred(key_of[1], (NP, PLEN, H), 1.0, 6.0, ((0, 128),))
    head = centred(key_of[2], (H, D), H ** -0.5, 0.21875)
    teacher = centred(key_of[3], (NQ, K), 2.0, 8.0, ((0, 128),), jnp.float32)
    cand_owner_keys = jax.random.split(jax.random.fold_in(key_of[4], 1), NQ // QDEV)
    cand_owner_turns = jax.random.permutation(jax.random.fold_in(key_of[4], 3), NQ // QDEV)
    cand_owner = jax.vmap(lambda own, number: shared_out(jax.random.fold_in(key_of[4], 2), own, number, QDEV, DEVICES, K, CAP, 2))(cand_owner_keys, cand_owner_turns).reshape((NQ, K))
    cand_local = with_ends(jax.random.randint(key_of[5], (NQ, K), 0, PDEV), jax.random.fold_in(key_of[5], 1), 0, PDEV - 1).astype(jnp.int32)
    query_lengths = uneven_parts(key_of[6], NQ, NQ * QLEN * 3 // 4, QLEN, 2).astype(jnp.int32)
    passage_lengths = uneven_parts(key_of[7], NP, NP * PLEN * 2 // 3, PLEN, 2).astype(jnp.int32)
    return {"query_states": query_states, "passage_states": passage_states, "head": head, "teacher": teacher, "cand_owner": cand_owner, "cand_local": cand_local, "query_lengths": query_lengths, "passage_lengths": passage_lengths}


SOFTMAX_TEMP = 0.05
EPSILON = 1e-06

def embed(states, head):
    flat_states = states.reshape(-1, states.shape[-1])
    projected = jnp.dot(flat_states, head, preferred_element_type=jnp.float32)
    norm_value = jnp.sqrt(lax.optimization_barrier(jnp.sum(projected * projected, axis=-1, keepdims=True)) + EPSILON)
    unit_rows = projected / norm_value
    embedded = unit_rows.astype(jnp.bfloat16).reshape(states.shape[0], states.shape[1], -1)
    return (lax.optimization_barrier(embedded), unit_rows, norm_value)

def head_term(states, unit_rows, norm_value, grads):
    flat_states = states.reshape(unit_rows.shape[0], -1)
    along = grads.reshape(unit_rows.shape)
    radial = lax.optimization_barrier(jnp.sum(along * unit_rows, axis=-1, keepdims=True))
    grad_pre = ((along - unit_rows * radial) / norm_value).astype(jnp.bfloat16)
    return jnp.dot(flat_states.T, grad_pre, preferred_element_type=jnp.float32)

def pair_terms(query_rows, passage_rows, passage_token_mask):
    token_similarity = jnp.einsum('id,kjd->kij', query_rows.astype(jnp.float32), passage_rows.astype(jnp.float32))
    exponent_terms = jnp.exp(token_similarity / SOFTMAX_TEMP) * passage_token_mask[:, None, :]
    return (exponent_terms, lax.optimization_barrier(jnp.sum(exponent_terms, axis=-1)))

def distill(scores, teacher):
    student_exp = jnp.exp(scores)
    student_sum = lax.optimization_barrier(jnp.sum(student_exp, axis=-1, keepdims=True))
    teacher_exp = jnp.exp(teacher)
    teacher_sum = lax.optimization_barrier(jnp.sum(teacher_exp, axis=-1, keepdims=True))
    target = teacher_exp / teacher_sum
    divergence = lax.optimization_barrier(jnp.sum(target * (teacher - jnp.log(teacher_sum) - (scores - jnp.log(student_sum))), axis=-1))
    return (student_exp / student_sum - target, divergence)

def reference(query_states, passage_states, head, teacher, cand_owner, cand_local, query_lengths, passage_lengths):
    query_emb, query_unit, query_norm = embed(query_states, head)
    passage_emb, passage_unit, passage_norm = embed(passage_states, head)
    cand_ids = (cand_owner * PDEV + cand_local).astype(jnp.int32)
    query_token_mask = (jnp.arange(QLEN, dtype=jnp.int32)[None, :] < query_lengths[:, None]).astype(jnp.float32)
    passage_token_mask = (jnp.arange(PLEN, dtype=jnp.int32)[None, :] < passage_lengths[:, None]).astype(jnp.float32)

    def forward_one(inputs):
        query_rows, row_mask_vector, picked = inputs
        exponent_terms, exponent_total = pair_terms(query_rows, passage_emb[picked], passage_token_mask[picked])
        return lax.optimization_barrier(jnp.sum(row_mask_vector[None, :] * (SOFTMAX_TEMP * jnp.log(exponent_total)), axis=-1))
    scores = lax.map(forward_one, (query_emb, query_token_mask, cand_ids))
    weights, divergence = distill(scores, teacher)
    loss = jnp.sum(divergence) / NQ

    def backward_one(carry, inputs):
        query_rows, row_mask_vector, picked, weight_row = inputs
        passage_rows = passage_emb[picked]
        exponent_terms, exponent_total = pair_terms(query_rows, passage_rows, passage_token_mask[picked])
        share = ((weight_row[:, None] * row_mask_vector[None, :] / exponent_total)[:, :, None] * exponent_terms).astype(jnp.bfloat16)
        share = lax.optimization_barrier(share).astype(jnp.float32)
        query_part = jnp.einsum('kij,kjd->kid', share, passage_rows.astype(jnp.float32)).astype(jnp.bfloat16)
        passage_part = jnp.einsum('kij,id->kjd', share, query_rows.astype(jnp.float32)).astype(jnp.bfloat16)
        query_part, passage_part = lax.optimization_barrier((query_part, passage_part))
        carry = carry.at[picked].add(passage_part.astype(jnp.float32))
        return (carry, lax.optimization_barrier(jnp.sum(query_part.astype(jnp.float32), axis=0)))
    passage_grad, query_grad = lax.scan(backward_one, jnp.zeros((NP, PLEN, D), jnp.float32), (query_emb, query_token_mask, cand_ids, weights))
    head_grad = head_term(query_states, query_unit, query_norm, query_grad) + head_term(passage_states, passage_unit, passage_norm, passage_grad)
    return (scores, loss, head_grad)
```

```python
import jax
import jax.numpy as jnp
from jax import lax
from jax.sharding import PartitionSpec as P

SOFTMAX_TEMP = 0.05
EPSILON = 1e-06
AXES = ("pb", "pa")
META = 128


def normalize(projected):
    norm_value = jnp.sqrt(jnp.sum(projected * projected, axis=-1, keepdims=True) + EPSILON)
    unit_rows = projected / norm_value
    return (unit_rows.astype(jnp.bfloat16), unit_rows, norm_value)


def grad_pre_of(unit_rows, norm_value, along):
    radial = jnp.sum(along * unit_rows, axis=-1, keepdims=True)
    return ((along - unit_rows * radial) / norm_value).astype(jnp.bfloat16)


def length_mask(lengths, width_value):
    return (jnp.arange(width_value, dtype=jnp.int32)[None, :] < lengths[:, None]).astype(
        jnp.float32
    )


def pair_terms(query_rows, passage_rows, passage_token_mask):
    token_similarity = jnp.einsum(
        "sid,sjd->sij", query_rows, passage_rows, preferred_element_type=jnp.float32
    )
    exponent_terms = jnp.exp(token_similarity / SOFTMAX_TEMP) * passage_token_mask[:, None, :]
    return (exponent_terms, jnp.sum(exponent_terms, axis=-1))


def pair_scores(exponent_total, query_token_mask):
    return jnp.sum(query_token_mask * (SOFTMAX_TEMP * jnp.log(exponent_total)), axis=-1)


def pair_grads(exponent_terms, exponent_total, query_token_mask, weights, query_rows, passage_rows):
    share = (
        (weights[:, None] * query_token_mask / exponent_total)[:, :, None] * exponent_terms
    ).astype(jnp.bfloat16)
    query_part = jnp.einsum(
        "sij,sjd->sid", share, passage_rows, preferred_element_type=jnp.float32
    ).astype(jnp.bfloat16)
    passage_part = jnp.einsum(
        "sij,sid->sjd", share, query_rows, preferred_element_type=jnp.float32
    ).astype(jnp.bfloat16)
    return (query_part, passage_part)


def distill(scores, teacher):
    student_exp = jnp.exp(scores)
    student_sum = jnp.sum(student_exp, axis=-1, keepdims=True)
    teacher_exp = jnp.exp(teacher)
    teacher_sum = jnp.sum(teacher_exp, axis=-1, keepdims=True)
    target = teacher_exp / teacher_sum
    divergence = jnp.sum(
        target * (teacher - jnp.log(teacher_sum) - (scores - jnp.log(student_sum))), axis=-1
    )
    return (student_exp / student_sum - target, divergence)


def exchange(values, devices):
    shaped = values.reshape((devices, -1) + values.shape[1:])
    moved = lax.all_to_all(shaped, AXES, split_axis=0, concat_axis=0, tiled=True)
    return moved.reshape(values.shape)


def all_sum(flat, devices):
    chunk = -(-flat.shape[0] // (devices * 128)) * 128
    padded = jnp.pad(flat, (0, devices * chunk - flat.shape[0]))
    gathered = lax.all_to_all(
        padded.reshape(devices, chunk), AXES, split_axis=0, concat_axis=0, tiled=True
    )
    reduced = jnp.sum(gathered, axis=0)
    spread = lax.all_to_all(
        jnp.broadcast_to(reduced[None], (devices, chunk)),
        AXES,
        split_axis=0,
        concat_axis=0,
        tiled=True,
    )
    return spread.reshape(-1)


def on_device(
    query_states,
    passage_states,
    head,
    teacher,
    cand_owner,
    cand_local,
    query_lengths,
    passage_lengths,
):
    devices = lax.axis_size("pb") * lax.axis_size("pa")
    queries, query_len, hidden = query_states.shape
    passages, passage_len, _ = passage_states.shape
    width = head.shape[1]
    candidates = cand_owner.shape[1]
    capacity = min(queries, max(2, 2 * queries * candidates // devices))
    slots = devices * capacity
    pairs = queries * candidates

    query_pre = jnp.einsum(
        "qih,hd->qid", query_states, head, preferred_element_type=jnp.float32
    )
    query_emb, query_unit, query_norm = normalize(query_pre)
    passage_pre = jnp.einsum(
        "pjh,hd->pjd", passage_states, head, preferred_element_type=jnp.float32
    )
    passage_emb, passage_unit, passage_norm = normalize(passage_pre)

    flat_owner = cand_owner.reshape(pairs)
    flat_local = cand_local.reshape(pairs)
    row_of = jnp.repeat(jnp.arange(queries, dtype=jnp.int32), candidates)
    same_owner = flat_owner[:, None] == flat_owner[None, :]
    earlier_row = row_of[None, :] < row_of[:, None]
    rank_value = jnp.sum((same_owner & earlier_row).astype(jnp.int32), axis=1)
    flat_slot = flat_owner * capacity + rank_value
    slot_pick = flat_slot[None, :] == jnp.arange(slots, dtype=jnp.int32)[:, None]
    slot_live = jnp.any(slot_pick, axis=1)
    slot_query = jnp.sum(jnp.where(slot_pick, row_of[None, :], 0), axis=1)
    slot_local = jnp.sum(jnp.where(slot_pick, flat_local[None, :], 0), axis=1)
    query_pick = (slot_query[:, None] == jnp.arange(queries, dtype=jnp.int32)[None, :]) & slot_live[
        :, None
    ]
    sent_len = jnp.sum(jnp.where(query_pick, query_lengths[None, :], 0), axis=1)
    sent_emb = jnp.dot(
        query_pick.astype(jnp.bfloat16),
        query_emb.reshape(queries, query_len * width),
        preferred_element_type=jnp.float32,
    ).astype(jnp.bfloat16)
    lane = jnp.arange(META, dtype=jnp.int32)[None, :]
    meta = jnp.where(
        lane == 0, slot_local[:, None], jnp.where(lane == 1, sent_len[:, None], 0)
    ).astype(jnp.bfloat16)
    payload = jnp.concatenate([sent_emb, meta], axis=1)
    got = exchange(payload, devices)
    recv_emb = got[:, : query_len * width].reshape(slots, query_len, width)
    recv_local = got[:, query_len * width].astype(jnp.int32)
    recv_len = got[:, query_len * width + 1].astype(jnp.int32)
    recv_mask = length_mask(recv_len, query_len)

    passage_pick = recv_local[:, None] == jnp.arange(passages, dtype=jnp.int32)[None, :]
    passage_rows = jnp.einsum(
        "sp,pjd->sjd",
        passage_pick.astype(jnp.bfloat16),
        passage_emb,
        preferred_element_type=jnp.float32,
    ).astype(jnp.bfloat16)
    picked_len = jnp.sum(jnp.where(passage_pick, passage_lengths[None, :], 0), axis=1)
    passage_token_mask = length_mask(picked_len, passage_len)
    exponent_terms, exponent_total = pair_terms(recv_emb, passage_rows, passage_token_mask)
    slot_scores = pair_scores(exponent_total, recv_mask)

    returned_scores = exchange(slot_scores, devices)
    scores = jnp.sum(jnp.where(slot_pick, returned_scores[:, None], 0.0), axis=0).reshape(
        queries, candidates
    )
    weights, divergence = distill(scores, teacher)
    sent_weight = jnp.sum(jnp.where(slot_pick, weights.reshape(pairs)[None, :], 0.0), axis=1)
    recv_weight = exchange(sent_weight, devices)

    query_part, passage_part = pair_grads(
        exponent_terms, exponent_total, recv_mask, recv_weight, recv_emb, passage_rows
    )
    passage_grad = jnp.einsum(
        "sp,sjd->pjd",
        passage_pick.astype(jnp.bfloat16),
        passage_part,
        preferred_element_type=jnp.float32,
    )
    returned_grads = exchange(query_part.reshape(slots, query_len * width), devices)
    query_grad = jnp.dot(
        query_pick.astype(jnp.bfloat16).T, returned_grads, preferred_element_type=jnp.float32
    ).reshape(queries, query_len, width)

    query_pre_grad = grad_pre_of(query_unit, query_norm, query_grad)
    passage_pre_grad = grad_pre_of(passage_unit, passage_norm, passage_grad)
    local_grad = jnp.einsum(
        "qih,qid->hd", query_states, query_pre_grad, preferred_element_type=jnp.float32
    ) + jnp.einsum(
        "pjh,pjd->hd", passage_states, passage_pre_grad, preferred_element_type=jnp.float32
    )
    flat = jnp.concatenate([local_grad.reshape(-1), jnp.sum(divergence)[None]])
    total = all_sum(flat, devices)
    head_grad = total[: hidden * width].reshape(hidden, width)
    loss = total[hidden * width] / (queries * devices)
    return (scores, loss, head_grad)


def solution(mesh):
    return jax.shard_map(
        on_device,
        mesh=mesh,
        in_specs=(
            P(AXES, None, None),
            P(AXES, None, None),
            P(),
            P(AXES, None),
            P(AXES, None),
            P(AXES, None),
            P(AXES),
            P(AXES),
        ),
        out_specs=(P(AXES, None), P(), P()),
        check_vma=False,
    )
```

```python
import jax
import jax.numpy as jnp
from jax import lax
from jax.sharding import PartitionSpec as P

SOFTMAX_TEMP = 0.05
EPSILON = 1e-06
AXES = ("pb", "pa")
META = 128


def normalize(projected):
    norm_value = jnp.sqrt(jnp.sum(projected * projected, axis=-1, keepdims=True) + EPSILON)
    unit_rows = projected / norm_value
    return (unit_rows.astype(jnp.bfloat16), unit_rows, norm_value)


def grad_pre_of(unit_rows, norm_value, along):
    radial = jnp.sum(along * unit_rows, axis=-1, keepdims=True)
    return ((along - unit_rows * radial) / norm_value).astype(jnp.bfloat16)


def length_mask(lengths, width_value):
    return (jnp.arange(width_value, dtype=jnp.int32)[None, :] < lengths[:, None]).astype(
        jnp.float32
    )


def pair_terms(query_rows, passage_rows, passage_token_mask):
    token_similarity = jnp.einsum(
        "sid,sjd->sij", query_rows, passage_rows, preferred_element_type=jnp.float32
    )
    exponent_terms = jnp.exp(token_similarity / SOFTMAX_TEMP) * passage_token_mask[:, None, :]
    return (exponent_terms, jnp.sum(exponent_terms, axis=-1))


def pair_scores(exponent_total, query_token_mask):
    return jnp.sum(query_token_mask * (SOFTMAX_TEMP * jnp.log(exponent_total)), axis=-1)


def pair_grads(exponent_terms, exponent_total, query_token_mask, weights, query_rows, passage_rows):
    share = (
        (weights[:, None] * query_token_mask / exponent_total)[:, :, None] * exponent_terms
    ).astype(jnp.bfloat16)
    query_part = jnp.einsum(
        "sij,sjd->sid", share, passage_rows, preferred_element_type=jnp.float32
    ).astype(jnp.bfloat16)
    passage_part = jnp.einsum(
        "sij,sid->sjd", share, query_rows, preferred_element_type=jnp.float32
    ).astype(jnp.bfloat16)
    return (query_part, passage_part)


def distill(scores, teacher):
    student_exp = jnp.exp(scores)
    student_sum = jnp.sum(student_exp, axis=-1, keepdims=True)
    teacher_exp = jnp.exp(teacher)
    teacher_sum = jnp.sum(teacher_exp, axis=-1, keepdims=True)
    target = teacher_exp / teacher_sum
    divergence = jnp.sum(
        target * (teacher - jnp.log(teacher_sum) - (scores - jnp.log(student_sum))), axis=-1
    )
    return (student_exp / student_sum - target, divergence)


def exchange(values, devices):
    shaped = values.reshape((devices, -1) + values.shape[1:])
    moved = lax.all_to_all(shaped, AXES, split_axis=0, concat_axis=0, tiled=True)
    return moved.reshape(values.shape)


def all_sum(flat, devices):
    chunk = -(-flat.shape[0] // (devices * 128)) * 128
    padded = jnp.pad(flat, (0, devices * chunk - flat.shape[0]))
    gathered = lax.all_to_all(
        padded.reshape(devices, chunk), AXES, split_axis=0, concat_axis=0, tiled=True
    )
    reduced = jnp.sum(gathered, axis=0)
    spread = lax.all_to_all(
        jnp.broadcast_to(reduced[None], (devices, chunk)),
        AXES,
        split_axis=0,
        concat_axis=0,
        tiled=True,
    )
    return spread.reshape(-1)


def on_device(
    query_states,
    passage_states,
    head,
    teacher,
    cand_owner,
    cand_local,
    query_lengths,
    passage_lengths,
):
    devices = lax.axis_size("pb") * lax.axis_size("pa")
    queries, query_len, hidden = query_states.shape
    passages, passage_len, _ = passage_states.shape
    width = head.shape[1]
    candidates = cand_owner.shape[1]
    capacity = min(queries, max(2, 2 * queries * candidates // devices))
    slots = devices * capacity
    pairs = queries * candidates

    query_flat = query_states.reshape(queries * query_len, hidden)
    query_pre = jnp.dot(query_flat, head, preferred_element_type=jnp.float32)
    query_emb, query_unit, query_norm = normalize(query_pre)
    passage_flat = jnp.transpose(passage_states, (1, 0, 2)).reshape(passage_len * passages, hidden)
    passage_pre = jnp.dot(passage_flat, head, preferred_element_type=jnp.float32)
    passage_emb_flat, passage_unit, passage_norm = normalize(passage_pre)
    passage_emb = jnp.transpose(passage_emb_flat.reshape(passage_len, passages, width), (1, 0, 2))

    flat_owner = cand_owner.reshape(pairs)
    flat_local = cand_local.reshape(pairs)
    row_of = jnp.repeat(jnp.arange(queries, dtype=jnp.int32), candidates)
    same_owner = flat_owner[:, None] == flat_owner[None, :]
    earlier_row = row_of[None, :] < row_of[:, None]
    rank_value = jnp.sum((same_owner & earlier_row).astype(jnp.int32), axis=1)
    flat_slot = flat_owner * capacity + rank_value
    slot_pick = flat_slot[None, :] == jnp.arange(slots, dtype=jnp.int32)[:, None]
    slot_live = jnp.any(slot_pick, axis=1)
    slot_query = jnp.sum(jnp.where(slot_pick, row_of[None, :], 0), axis=1)
    slot_local = jnp.sum(jnp.where(slot_pick, flat_local[None, :], 0), axis=1)
    query_pick = (slot_query[:, None] == jnp.arange(queries, dtype=jnp.int32)[None, :]) & slot_live[
        :, None
    ]
    sent_len = jnp.sum(jnp.where(query_pick, query_lengths[None, :], 0), axis=1)
    sent_emb = jnp.dot(
        query_pick.astype(jnp.bfloat16),
        query_emb.reshape(queries, query_len * width),
        preferred_element_type=jnp.float32,
    ).astype(jnp.bfloat16)
    lane = jnp.arange(META, dtype=jnp.int32)[None, :]
    meta = jnp.where(
        lane == 0, slot_local[:, None], jnp.where(lane == 1, sent_len[:, None], 0)
    ).astype(jnp.bfloat16)
    payload = jnp.concatenate([sent_emb, meta], axis=1)
    got = exchange(payload, devices)
    recv_emb = got[:, : query_len * width].reshape(slots, query_len, width)
    recv_local = got[:, query_len * width].astype(jnp.int32)
    recv_len = got[:, query_len * width + 1].astype(jnp.int32)
    recv_mask = length_mask(recv_len, query_len)

    passage_pick = recv_local[:, None] == jnp.arange(passages, dtype=jnp.int32)[None, :]
    passage_rows = jnp.einsum(
        "sp,pjd->sjd",
        passage_pick.astype(jnp.bfloat16),
        passage_emb,
        preferred_element_type=jnp.float32,
    ).astype(jnp.bfloat16)
    picked_len = jnp.sum(jnp.where(passage_pick, passage_lengths[None, :], 0), axis=1)
    passage_token_mask = length_mask(picked_len, passage_len)
    exponent_terms, exponent_total = pair_terms(recv_emb, passage_rows, passage_token_mask)
    slot_scores = pair_scores(exponent_total, recv_mask)

    returned_scores = exchange(slot_scores, devices)
    scores = jnp.sum(jnp.where(slot_pick, returned_scores[:, None], 0.0), axis=0).reshape(
        queries, candidates
    )
    weights, divergence = distill(scores, teacher)
    sent_weight = jnp.sum(jnp.where(slot_pick, weights.reshape(pairs)[None, :], 0.0), axis=1)
    recv_weight = exchange(sent_weight, devices)

    query_part, passage_part = pair_grads(
        exponent_terms, exponent_total, recv_mask, recv_weight, recv_emb, passage_rows
    )
    passage_grad = jnp.einsum(
        "sp,sjd->jpd",
        passage_pick.astype(jnp.bfloat16),
        passage_part,
        preferred_element_type=jnp.float32,
    )
    returned_grads = exchange(query_part.reshape(slots, query_len * width), devices)
    query_grad = jnp.dot(
        query_pick.astype(jnp.bfloat16).T, returned_grads, preferred_element_type=jnp.float32
    ).reshape(queries, query_len, width)

    query_pre_grad = grad_pre_of(query_unit, query_norm, query_grad.reshape(queries * query_len, width))
    passage_pre_grad = grad_pre_of(
        passage_unit, passage_norm, passage_grad.reshape(passage_len * passages, width)
    )
    contract = (((0,), (0,)), ((), ()))
    local_grad = lax.dot_general(
        query_flat, query_pre_grad, contract, preferred_element_type=jnp.float32
    ) + lax.dot_general(passage_flat, passage_pre_grad, contract, preferred_element_type=jnp.float32)
    flat = jnp.concatenate([local_grad.reshape(-1), jnp.sum(divergence)[None]])
    total = all_sum(flat, devices)
    head_grad = total[: hidden * width].reshape(hidden, width)
    loss = total[hidden * width] / (queries * devices)
    return (scores, loss, head_grad)


def solution(mesh):
    return jax.shard_map(
        on_device,
        mesh=mesh,
        in_specs=(
            P(AXES, None, None),
            P(AXES, None, None),
            P(),
            P(AXES, None),
            P(AXES, None),
            P(AXES, None),
            P(AXES),
            P(AXES),
        ),
        out_specs=(P(AXES, None), P(), P()),
        check_vma=False,
    )
```

```python
import jax
import jax.numpy as jnp
from jax import lax
from jax.sharding import PartitionSpec as P

SOFTMAX_TEMP = 0.05
EPSILON = 1e-06
AXES = ("pb", "pa")
META = 128


def normalize(projected):
    norm_value = jnp.sqrt(jnp.sum(projected * projected, axis=-1, keepdims=True) + EPSILON)
    unit_rows = projected / norm_value
    return (unit_rows.astype(jnp.bfloat16), unit_rows, norm_value)


def grad_pre_of(unit_rows, norm_value, along):
    radial = jnp.sum(along * unit_rows, axis=-1, keepdims=True)
    return ((along - unit_rows * radial) / norm_value).astype(jnp.bfloat16)


def length_mask(lengths, width_value):
    return (jnp.arange(width_value, dtype=jnp.int32)[None, :] < lengths[:, None]).astype(
        jnp.float32
    )


def pair_terms(query_rows, passage_rows, passage_token_mask):
    token_similarity = jnp.einsum(
        "sid,sjd->sij", query_rows, passage_rows, preferred_element_type=jnp.float32
    )
    exponent_terms = jnp.exp(token_similarity / SOFTMAX_TEMP) * passage_token_mask[:, None, :]
    return (exponent_terms, jnp.sum(exponent_terms, axis=-1))


def pair_scores(exponent_total, query_token_mask):
    return jnp.sum(query_token_mask * (SOFTMAX_TEMP * jnp.log(exponent_total)), axis=-1)


def pair_grads(exponent_terms, exponent_total, query_token_mask, weights, query_rows, passage_rows):
    share = (
        (weights[:, None] * query_token_mask / exponent_total)[:, :, None] * exponent_terms
    ).astype(jnp.bfloat16)
    query_part = jnp.einsum(
        "sij,sjd->sid", share, passage_rows, preferred_element_type=jnp.float32
    ).astype(jnp.bfloat16)
    passage_part = jnp.einsum(
        "sij,sid->sjd", share, query_rows, preferred_element_type=jnp.float32
    ).astype(jnp.bfloat16)
    return (query_part, passage_part)


def distill(scores, teacher):
    student_exp = jnp.exp(scores)
    student_sum = jnp.sum(student_exp, axis=-1, keepdims=True)
    teacher_exp = jnp.exp(teacher)
    teacher_sum = jnp.sum(teacher_exp, axis=-1, keepdims=True)
    target = teacher_exp / teacher_sum
    divergence = jnp.sum(
        target * (teacher - jnp.log(teacher_sum) - (scores - jnp.log(student_sum))), axis=-1
    )
    return (student_exp / student_sum - target, divergence)


def exchange(values, devices):
    shaped = values.reshape((devices, -1) + values.shape[1:])
    moved = lax.all_to_all(shaped, AXES, split_axis=0, concat_axis=0, tiled=True)
    return moved.reshape(values.shape)


def all_sum(flat, devices):
    chunk = -(-flat.shape[0] // (devices * 128)) * 128
    padded = jnp.pad(flat, (0, devices * chunk - flat.shape[0]))
    gathered = lax.all_to_all(
        padded.reshape(devices, chunk), AXES, split_axis=0, concat_axis=0, tiled=True
    )
    reduced = jnp.sum(gathered, axis=0)
    spread = lax.all_to_all(
        jnp.broadcast_to(reduced[None], (devices, chunk)),
        AXES,
        split_axis=0,
        concat_axis=0,
        tiled=True,
    )
    return spread.reshape(-1)


def on_device(
    query_states,
    passage_states,
    head,
    teacher,
    cand_owner,
    cand_local,
    query_lengths,
    passage_lengths,
):
    devices = lax.axis_size("pb") * lax.axis_size("pa")
    queries, query_len, hidden = query_states.shape
    passages, passage_len, _ = passage_states.shape
    width = head.shape[1]
    candidates = cand_owner.shape[1]
    capacity = min(queries, max(2, 2 * queries * candidates // devices))
    slots = devices * capacity
    pairs = queries * candidates

    query_flat = query_states.reshape(queries * query_len, hidden)
    query_pre = jnp.dot(query_flat, head, preferred_element_type=jnp.float32)
    query_emb, query_unit, query_norm = normalize(query_pre)
    passage_flat = jnp.transpose(passage_states, (1, 0, 2)).reshape(passage_len * passages, hidden)
    passage_pre = jnp.dot(passage_flat, head, preferred_element_type=jnp.float32)
    passage_emb_flat, passage_unit, passage_norm = normalize(passage_pre)
    passage_emb = jnp.transpose(passage_emb_flat.reshape(passage_len, passages, width), (1, 0, 2))

    flat_owner = cand_owner.reshape(pairs)
    flat_local = cand_local.reshape(pairs)
    row_of = jnp.repeat(jnp.arange(queries, dtype=jnp.int32), candidates)
    k_of = jnp.tile(jnp.arange(candidates, dtype=jnp.int32), queries)
    same_owner = flat_owner[:, None] == flat_owner[None, :]
    earlier_row = row_of[None, :] < row_of[:, None]
    rank_value = jnp.sum((same_owner & earlier_row).astype(jnp.int32), axis=1)
    flat_slot = flat_owner * capacity + rank_value
    slot_pick = flat_slot[None, :] == jnp.arange(slots, dtype=jnp.int32)[:, None]
    slot_live = jnp.any(slot_pick, axis=1)
    slot_query = jnp.sum(jnp.where(slot_pick, row_of[None, :], 0), axis=1)
    slot_k = jnp.sum(jnp.where(slot_pick, k_of[None, :], 0), axis=1)
    slot_local = jnp.sum(jnp.where(slot_pick, flat_local[None, :], 0), axis=1)
    query_pick = (slot_query[:, None] == jnp.arange(queries, dtype=jnp.int32)[None, :]) & slot_live[
        :, None
    ]
    sent_len = jnp.sum(jnp.where(query_pick, query_lengths[None, :], 0), axis=1)
    owner_rows = jnp.sum(jnp.where(query_pick[:, :, None], cand_owner[None], 0), axis=1)
    rank_rows = jnp.sum(
        jnp.where(query_pick[:, :, None], rank_value.reshape(queries, candidates)[None], 0), axis=1
    )
    sent_emb = jnp.dot(
        query_pick.astype(jnp.bfloat16),
        query_emb.reshape(queries, query_len * width),
        preferred_element_type=jnp.float32,
    ).astype(jnp.bfloat16)
    scalars = jnp.stack([slot_local, sent_len, slot_query, slot_k], axis=1)
    meta = jnp.concatenate(
        [
            scalars,
            jnp.zeros((slots, META - 4 - 2 * candidates), jnp.int32),
            owner_rows,
            rank_rows,
        ],
        axis=1,
    ).astype(jnp.bfloat16)
    payload = jnp.concatenate([sent_emb, meta], axis=1)
    got = exchange(payload, devices)
    recv_emb = got[:, : query_len * width].reshape(slots, query_len, width)
    recv_meta = got[:, query_len * width :].astype(jnp.int32)
    recv_local = recv_meta[:, 0]
    recv_len = recv_meta[:, 1]
    recv_query = recv_meta[:, 2]
    recv_k = recv_meta[:, 3]
    recv_owner = recv_meta[:, META - 2 * candidates : META - candidates]
    recv_rank = recv_meta[:, META - candidates :]
    recv_mask = length_mask(recv_len, query_len)

    passage_pick = recv_local[:, None] == jnp.arange(passages, dtype=jnp.int32)[None, :]
    passage_rows = jnp.einsum(
        "sp,pjd->sjd",
        passage_pick.astype(jnp.bfloat16),
        passage_emb,
        preferred_element_type=jnp.float32,
    ).astype(jnp.bfloat16)
    picked_len = jnp.sum(jnp.where(passage_pick, passage_lengths[None, :], 0), axis=1)
    passage_token_mask = length_mask(picked_len, passage_len)
    exponent_terms, exponent_total = pair_terms(recv_emb, passage_rows, passage_token_mask)
    slot_scores = pair_scores(exponent_total, recv_mask)

    teacher_exp = jnp.exp(teacher)
    target = teacher_exp / jnp.sum(teacher_exp, axis=-1, keepdims=True)
    shared = jnp.concatenate([slot_scores, target.reshape(pairs)])
    table = lax.all_to_all(
        jnp.broadcast_to(shared[None], (devices, slots + pairs)),
        AXES,
        split_axis=0,
        concat_axis=0,
        tiled=True,
    )
    score_table = table[:, :slots].reshape(devices, devices, capacity)
    by_source = jnp.transpose(score_table, (1, 0, 2)).reshape(devices, devices * capacity)
    by_slot = jnp.repeat(by_source, capacity, axis=0)
    column = jnp.arange(devices * capacity, dtype=jnp.int32)
    row_column = recv_owner * capacity + recv_rank
    row_scores = jnp.sum(
        jnp.where(column[None, None, :] == row_column[:, :, None], by_slot[:, None, :], 0.0), axis=2
    )
    target_rows = jnp.repeat(table[:, slots:], capacity, axis=0)
    target_column = recv_query * candidates + recv_k
    slot_target = jnp.sum(
        jnp.where(
            jnp.arange(pairs, dtype=jnp.int32)[None, :] == target_column[:, None], target_rows, 0.0
        ),
        axis=1,
    )
    student_sum = jnp.sum(jnp.exp(row_scores), axis=-1)
    recv_weight = jnp.where(recv_len > 0, jnp.exp(slot_scores) / student_sum - slot_target, 0.0)

    me = lax.axis_index(AXES)
    mine = lax.dynamic_slice_in_dim(score_table, me, 1, axis=1).reshape(devices * capacity)
    scores = jnp.sum(
        jnp.where(column[None, :] == flat_slot[:, None], mine[None, :], 0.0), axis=1
    ).reshape(queries, candidates)
    _, divergence = distill(scores, teacher)

    query_part, passage_part = pair_grads(
        exponent_terms, exponent_total, recv_mask, recv_weight, recv_emb, passage_rows
    )
    passage_grad = jnp.einsum(
        "sp,sjd->jpd",
        passage_pick.astype(jnp.bfloat16),
        passage_part,
        preferred_element_type=jnp.float32,
    )
    returned_grads = exchange(query_part.reshape(slots, query_len * width), devices)
    query_grad = jnp.dot(
        query_pick.astype(jnp.bfloat16).T, returned_grads, preferred_element_type=jnp.float32
    ).reshape(queries, query_len, width)

    query_pre_grad = grad_pre_of(query_unit, query_norm, query_grad.reshape(queries * query_len, width))
    passage_pre_grad = grad_pre_of(
        passage_unit, passage_norm, passage_grad.reshape(passage_len * passages, width)
    )
    contract = (((0,), (0,)), ((), ()))
    local_grad = lax.dot_general(
        query_flat, query_pre_grad, contract, preferred_element_type=jnp.float32
    ) + lax.dot_general(passage_flat, passage_pre_grad, contract, preferred_element_type=jnp.float32)
    flat = jnp.concatenate([local_grad.reshape(-1), jnp.sum(divergence)[None]])
    total = all_sum(flat, devices)
    head_grad = total[: hidden * width].reshape(hidden, width)
    loss = total[hidden * width] / (queries * devices)
    return (scores, loss, head_grad)


def solution(mesh):
    return jax.shard_map(
        on_device,
        mesh=mesh,
        in_specs=(
            P(AXES, None, None),
            P(AXES, None, None),
            P(),
            P(AXES, None),
            P(AXES, None),
            P(AXES, None),
            P(AXES),
            P(AXES),
        ),
        out_specs=(P(AXES, None), P(), P()),
        check_vma=False,
    )
```

```python
import jax
import jax.numpy as jnp
from jax import lax
from jax.sharding import PartitionSpec as P

SOFTMAX_TEMP = 0.05
EPSILON = 1e-06
AXES = ("pb", "pa")
META = 128


def normalize(projected):
    norm_value = jnp.sqrt(jnp.sum(projected * projected, axis=-1, keepdims=True) + EPSILON)
    unit_rows = projected / norm_value
    return (unit_rows.astype(jnp.bfloat16), unit_rows, norm_value)


def grad_pre_of(unit_rows, norm_value, along):
    radial = jnp.sum(along * unit_rows, axis=-1, keepdims=True)
    return ((along - unit_rows * radial) / norm_value).astype(jnp.bfloat16)


def length_mask(lengths, width_value):
    return (jnp.arange(width_value, dtype=jnp.int32)[None, :] < lengths[:, None]).astype(
        jnp.float32
    )


def pair_terms(query_rows, passage_rows, passage_token_mask):
    token_similarity = jnp.einsum(
        "sid,sjd->sij", query_rows, passage_rows, preferred_element_type=jnp.float32
    )
    exponent_terms = jnp.exp(token_similarity / SOFTMAX_TEMP) * passage_token_mask[:, None, :]
    return (exponent_terms, jnp.sum(exponent_terms, axis=-1))


def pair_scores(exponent_total, query_token_mask):
    return jnp.sum(query_token_mask * (SOFTMAX_TEMP * jnp.log(exponent_total)), axis=-1)


def pair_grads(exponent_terms, exponent_total, query_token_mask, weights, query_rows, passage_rows):
    share = (
        (weights[:, None] * query_token_mask / exponent_total)[:, :, None] * exponent_terms
    ).astype(jnp.bfloat16)
    query_part = jnp.einsum(
        "sij,sjd->sid", share, passage_rows, preferred_element_type=jnp.float32
    ).astype(jnp.bfloat16)
    passage_part = jnp.einsum(
        "sij,sid->sjd", share, query_rows, preferred_element_type=jnp.float32
    ).astype(jnp.bfloat16)
    return (query_part, passage_part)


def distill(scores, teacher):
    student_exp = jnp.exp(scores)
    student_sum = jnp.sum(student_exp, axis=-1, keepdims=True)
    teacher_exp = jnp.exp(teacher)
    teacher_sum = jnp.sum(teacher_exp, axis=-1, keepdims=True)
    target = teacher_exp / teacher_sum
    divergence = jnp.sum(
        target * (teacher - jnp.log(teacher_sum) - (scores - jnp.log(student_sum))), axis=-1
    )
    return (student_exp / student_sum - target, divergence)


def exchange(values, devices):
    shaped = values.reshape((devices, -1) + values.shape[1:])
    moved = lax.all_to_all(shaped, AXES, split_axis=0, concat_axis=0, tiled=True)
    return moved.reshape(values.shape)


def all_sum(flat, devices):
    chunk = -(-flat.shape[0] // (devices * 128)) * 128
    padded = jnp.pad(flat, (0, devices * chunk - flat.shape[0]))
    gathered = lax.all_to_all(
        padded.reshape(devices, chunk), AXES, split_axis=0, concat_axis=0, tiled=True
    )
    reduced = jnp.sum(gathered, axis=0)
    spread = lax.all_to_all(
        jnp.broadcast_to(reduced[None], (devices, chunk)),
        AXES,
        split_axis=0,
        concat_axis=0,
        tiled=True,
    )
    return spread.reshape(-1)


def on_device(
    query_states,
    passage_states,
    head,
    teacher,
    cand_owner,
    cand_local,
    query_lengths,
    passage_lengths,
):
    devices = lax.axis_size("pb") * lax.axis_size("pa")
    queries, query_len, hidden = query_states.shape
    passages, passage_len, _ = passage_states.shape
    width = head.shape[1]
    candidates = cand_owner.shape[1]
    capacity = min(queries, max(2, 2 * queries * candidates // devices))
    slots = devices * capacity
    pairs = queries * candidates

    query_flat = query_states.reshape(queries * query_len, hidden)
    query_pre = jnp.dot(query_flat, head, preferred_element_type=jnp.float32)
    query_emb, query_unit, query_norm = normalize(query_pre)
    passage_flat = jnp.transpose(passage_states, (1, 0, 2)).reshape(passage_len * passages, hidden)
    passage_pre = jnp.dot(passage_flat, head, preferred_element_type=jnp.float32)
    passage_emb_flat, passage_unit, passage_norm = normalize(passage_pre)
    passage_emb = jnp.transpose(passage_emb_flat.reshape(passage_len, passages, width), (1, 0, 2))

    flat_owner = cand_owner.reshape(pairs)
    flat_local = cand_local.reshape(pairs)
    row_of = jnp.repeat(jnp.arange(queries, dtype=jnp.int32), candidates)
    k_of = jnp.tile(jnp.arange(candidates, dtype=jnp.int32), queries)
    same_owner = flat_owner[:, None] == flat_owner[None, :]
    earlier_row = row_of[None, :] < row_of[:, None]
    rank_value = jnp.sum((same_owner & earlier_row).astype(jnp.int32), axis=1)
    flat_slot = flat_owner * capacity + rank_value
    slot_pick = flat_slot[None, :] == jnp.arange(slots, dtype=jnp.int32)[:, None]
    slot_live = jnp.any(slot_pick, axis=1)
    slot_query = jnp.sum(jnp.where(slot_pick, row_of[None, :], 0), axis=1)
    slot_k = jnp.sum(jnp.where(slot_pick, k_of[None, :], 0), axis=1)
    slot_local = jnp.sum(jnp.where(slot_pick, flat_local[None, :], 0), axis=1)
    query_pick = (slot_query[:, None] == jnp.arange(queries, dtype=jnp.int32)[None, :]) & slot_live[
        :, None
    ]
    sent_len = jnp.sum(jnp.where(query_pick, query_lengths[None, :], 0), axis=1)
    sent_emb = jnp.dot(
        query_pick.astype(jnp.bfloat16),
        query_emb.reshape(queries, query_len * width),
        preferred_element_type=jnp.float32,
    ).astype(jnp.bfloat16)
    lane = jnp.arange(META, dtype=jnp.int32)[None, :]
    meta = jnp.where(
        lane == 0,
        slot_local[:, None],
        jnp.where(
            lane == 1,
            sent_len[:, None],
            jnp.where(lane == 2, slot_query[:, None], jnp.where(lane == 3, slot_k[:, None], 0)),
        ),
    ).astype(jnp.bfloat16)
    payload = jnp.concatenate([sent_emb, meta], axis=1)
    got = exchange(payload, devices)
    recv_emb = got[:, : query_len * width].reshape(slots, query_len, width)
    recv_meta = got[:, query_len * width : query_len * width + 4].astype(jnp.int32)
    recv_local = recv_meta[:, 0]
    recv_len = recv_meta[:, 1]
    recv_query = recv_meta[:, 2]
    recv_k = recv_meta[:, 3]
    recv_mask = length_mask(recv_len, query_len)

    passage_pick = recv_local[:, None] == jnp.arange(passages, dtype=jnp.int32)[None, :]
    passage_rows = jnp.einsum(
        "sp,pjd->sjd",
        passage_pick.astype(jnp.bfloat16),
        passage_emb,
        preferred_element_type=jnp.float32,
    ).astype(jnp.bfloat16)
    picked_len = jnp.sum(jnp.where(passage_pick, passage_lengths[None, :], 0), axis=1)
    passage_token_mask = length_mask(picked_len, passage_len)
    exponent_terms, exponent_total = pair_terms(recv_emb, passage_rows, passage_token_mask)
    slot_scores = pair_scores(exponent_total, recv_mask)

    teacher_exp = jnp.exp(teacher)
    target = teacher_exp / jnp.sum(teacher_exp, axis=-1, keepdims=True)
    recv_label = jnp.where(recv_len > 0, recv_query, -1).astype(jnp.float32)
    shared = jnp.concatenate([slot_scores, recv_label, target.reshape(pairs)])
    table = lax.all_to_all(
        jnp.broadcast_to(shared[None], (devices, 2 * slots + pairs)),
        AXES,
        split_axis=0,
        concat_axis=0,
        tiled=True,
    )
    score_table = table[:, :slots].reshape(devices, devices, capacity)
    label_table = table[:, slots : 2 * slots].reshape(devices, devices, capacity)
    query_ids = jnp.arange(queries, dtype=jnp.float32)
    query_sums = jnp.sum(
        jnp.where(
            label_table[:, :, :, None] == query_ids, jnp.exp(score_table)[:, :, :, None], 0.0
        ),
        axis=(0, 2),
    )
    slot_sums = jnp.repeat(query_sums, capacity, axis=0)
    student_sum = jnp.sum(
        jnp.where(
            recv_query[:, None] == jnp.arange(queries, dtype=jnp.int32)[None, :], slot_sums, 0.0
        ),
        axis=1,
    )
    target_rows = jnp.repeat(table[:, 2 * slots :], capacity, axis=0)
    target_column = recv_query * candidates + recv_k
    slot_target = jnp.sum(
        jnp.where(
            jnp.arange(pairs, dtype=jnp.int32)[None, :] == target_column[:, None], target_rows, 0.0
        ),
        axis=1,
    )
    recv_weight = jnp.where(recv_len > 0, jnp.exp(slot_scores) / student_sum - slot_target, 0.0)

    column = jnp.arange(devices * capacity, dtype=jnp.int32)
    me = lax.axis_index(AXES)
    mine = lax.dynamic_slice_in_dim(score_table, me, 1, axis=1).reshape(devices * capacity)
    scores = jnp.sum(
        jnp.where(column[None, :] == flat_slot[:, None], mine[None, :], 0.0), axis=1
    ).reshape(queries, candidates)
    _, divergence = distill(scores, teacher)

    query_part, passage_part = pair_grads(
        exponent_terms, exponent_total, recv_mask, recv_weight, recv_emb, passage_rows
    )
    passage_grad = jnp.einsum(
        "sp,sjd->jpd",
        passage_pick.astype(jnp.bfloat16),
        passage_part,
        preferred_element_type=jnp.float32,
    )
    returned_grads = exchange(query_part.reshape(slots, query_len * width), devices)
    query_grad = jnp.dot(
        query_pick.astype(jnp.bfloat16).T, returned_grads, preferred_element_type=jnp.float32
    ).reshape(queries, query_len, width)

    query_pre_grad = grad_pre_of(query_unit, query_norm, query_grad.reshape(queries * query_len, width))
    passage_pre_grad = grad_pre_of(
        passage_unit, passage_norm, passage_grad.reshape(passage_len * passages, width)
    )
    contract = (((0,), (0,)), ((), ()))
    local_grad = lax.dot_general(
        query_flat, query_pre_grad, contract, preferred_element_type=jnp.float32
    ) + lax.dot_general(passage_flat, passage_pre_grad, contract, preferred_element_type=jnp.float32)
    flat = jnp.concatenate([local_grad.reshape(-1), jnp.sum(divergence)[None]])
    total = all_sum(flat, devices)
    head_grad = total[: hidden * width].reshape(hidden, width)
    loss = total[hidden * width] / (queries * devices)
    return (scores, loss, head_grad)


def solution(mesh):
    return jax.shard_map(
        on_device,
        mesh=mesh,
        in_specs=(
            P(AXES, None, None),
            P(AXES, None, None),
            P(),
            P(AXES, None),
            P(AXES, None),
            P(AXES, None),
            P(AXES),
            P(AXES),
        ),
        out_specs=(P(AXES, None), P(), P()),
        check_vma=False,
    )
```

```python
import jax
import jax.numpy as jnp
from jax import lax
from jax.sharding import PartitionSpec as P

SOFTMAX_TEMP = 0.05
EPSILON = 1e-06
AXES = ("pb", "pa")
META = 128


def normalize(projected):
    norm_value = jnp.sqrt(jnp.sum(projected * projected, axis=-1, keepdims=True) + EPSILON)
    unit_rows = projected / norm_value
    return (unit_rows.astype(jnp.bfloat16), unit_rows, norm_value)


def grad_pre_of(unit_rows, norm_value, along):
    radial = jnp.sum(along * unit_rows, axis=-1, keepdims=True)
    return ((along - unit_rows * radial) / norm_value).astype(jnp.bfloat16)


def length_mask(lengths, width_value):
    return (jnp.arange(width_value, dtype=jnp.int32)[None, :] < lengths[:, None]).astype(
        jnp.float32
    )


def pair_terms(query_rows, passage_rows, passage_token_mask):
    token_similarity = jnp.einsum(
        "sid,sjd->sij", query_rows, passage_rows, preferred_element_type=jnp.float32
    )
    exponent_terms = jnp.exp(token_similarity / SOFTMAX_TEMP) * passage_token_mask[:, None, :]
    return (exponent_terms, jnp.sum(exponent_terms, axis=-1))


def pair_scores(exponent_total, query_token_mask):
    return jnp.sum(query_token_mask * (SOFTMAX_TEMP * jnp.log(exponent_total)), axis=-1)


def pair_grads(exponent_terms, exponent_total, query_token_mask, weights, query_rows, passage_rows):
    share = (
        (weights[:, None] * query_token_mask / exponent_total)[:, :, None] * exponent_terms
    ).astype(jnp.bfloat16)
    query_part = jnp.einsum(
        "sij,sjd->sid", share, passage_rows, preferred_element_type=jnp.float32
    ).astype(jnp.bfloat16)
    passage_part = jnp.einsum(
        "sij,sid->sjd", share, query_rows, preferred_element_type=jnp.float32
    ).astype(jnp.bfloat16)
    return (query_part, passage_part)


def distill(scores, teacher):
    student_exp = jnp.exp(scores)
    student_sum = jnp.sum(student_exp, axis=-1, keepdims=True)
    teacher_exp = jnp.exp(teacher)
    teacher_sum = jnp.sum(teacher_exp, axis=-1, keepdims=True)
    target = teacher_exp / teacher_sum
    divergence = jnp.sum(
        target * (teacher - jnp.log(teacher_sum) - (scores - jnp.log(student_sum))), axis=-1
    )
    return (student_exp / student_sum - target, divergence)


def exchange(values, devices):
    shaped = values.reshape((devices, -1) + values.shape[1:])
    moved = lax.all_to_all(shaped, AXES, split_axis=0, concat_axis=0, tiled=True)
    return moved.reshape(values.shape)


def all_sum(flat, devices):
    chunk = -(-flat.shape[0] // (devices * 128)) * 128
    padded = jnp.pad(flat, (0, devices * chunk - flat.shape[0]))
    gathered = lax.all_to_all(
        padded.reshape(devices, chunk), AXES, split_axis=0, concat_axis=0, tiled=True
    )
    reduced = jnp.sum(gathered, axis=0)
    spread = lax.all_to_all(
        jnp.broadcast_to(reduced[None], (devices, chunk)),
        AXES,
        split_axis=0,
        concat_axis=0,
        tiled=True,
    )
    return spread.reshape(-1)


def on_device(
    query_states,
    passage_states,
    head,
    teacher,
    cand_owner,
    cand_local,
    query_lengths,
    passage_lengths,
):
    devices = lax.axis_size("pb") * lax.axis_size("pa")
    queries, query_len, hidden = query_states.shape
    passages, passage_len, _ = passage_states.shape
    width = head.shape[1]
    candidates = cand_owner.shape[1]
    capacity = min(queries, max(2, 2 * queries * candidates // devices))
    slots = devices * capacity
    pairs = queries * candidates

    query_flat = query_states.reshape(queries * query_len, hidden)
    query_pre = jnp.dot(query_flat, head, preferred_element_type=jnp.float32)
    query_emb, query_unit, query_norm = normalize(query_pre)
    passage_flat = jnp.transpose(passage_states, (1, 0, 2)).reshape(passage_len * passages, hidden)
    passage_pre = jnp.dot(passage_flat, head, preferred_element_type=jnp.float32)
    passage_emb_flat, passage_unit, passage_norm = normalize(passage_pre)
    passage_emb = jnp.transpose(passage_emb_flat.reshape(passage_len, passages, width), (1, 0, 2))

    flat_owner = cand_owner.reshape(pairs)
    flat_local = cand_local.reshape(pairs)
    row_of = jnp.repeat(jnp.arange(queries, dtype=jnp.int32), candidates)
    k_of = jnp.tile(jnp.arange(candidates, dtype=jnp.int32), queries)
    same_owner = flat_owner[:, None] == flat_owner[None, :]
    earlier_row = row_of[None, :] < row_of[:, None]
    rank_value = jnp.sum((same_owner & earlier_row).astype(jnp.int32), axis=1)
    flat_slot = flat_owner * capacity + rank_value
    slot_pick = flat_slot[None, :] == jnp.arange(slots, dtype=jnp.int32)[:, None]
    slot_live = jnp.any(slot_pick, axis=1)
    slot_query = jnp.sum(jnp.where(slot_pick, row_of[None, :], 0), axis=1)
    slot_k = jnp.sum(jnp.where(slot_pick, k_of[None, :], 0), axis=1)
    slot_local = jnp.sum(jnp.where(slot_pick, flat_local[None, :], 0), axis=1)
    query_pick = (slot_query[:, None] == jnp.arange(queries, dtype=jnp.int32)[None, :]) & slot_live[
        :, None
    ]
    sent_len = jnp.sum(jnp.where(query_pick, query_lengths[None, :], 0), axis=1)
    sent_emb = jnp.dot(
        query_pick.astype(jnp.bfloat16),
        query_emb.reshape(queries, query_len * width),
        preferred_element_type=jnp.float32,
    ).astype(jnp.bfloat16)
    lane = jnp.arange(META, dtype=jnp.int32)[None, :]
    meta = jnp.where(
        lane == 0,
        slot_local[:, None],
        jnp.where(
            lane == 1,
            sent_len[:, None],
            jnp.where(lane == 2, slot_query[:, None], jnp.where(lane == 3, slot_k[:, None], 0)),
        ),
    ).astype(jnp.bfloat16)
    payload = jnp.concatenate([sent_emb, meta], axis=1)
    got = exchange(payload, devices)
    recv_emb = got[:, : query_len * width].reshape(slots, query_len, width)
    recv_meta = got[:, query_len * width : query_len * width + 4].astype(jnp.int32)
    recv_local = recv_meta[:, 0]
    recv_len = recv_meta[:, 1]
    recv_query = recv_meta[:, 2]
    recv_k = recv_meta[:, 3]
    recv_mask = length_mask(recv_len, query_len)

    passage_pick = recv_local[:, None] == jnp.arange(passages, dtype=jnp.int32)[None, :]
    passage_rows = jnp.einsum(
        "sp,pjd->sjd",
        passage_pick.astype(jnp.bfloat16),
        passage_emb,
        preferred_element_type=jnp.float32,
    ).astype(jnp.bfloat16)
    picked_len = jnp.sum(jnp.where(passage_pick, passage_lengths[None, :], 0), axis=1)
    passage_token_mask = length_mask(picked_len, passage_len)
    exponent_terms, exponent_total = pair_terms(recv_emb, passage_rows, passage_token_mask)
    slot_scores = pair_scores(exponent_total, recv_mask)

    teacher_exp = jnp.exp(teacher)
    target = teacher_exp / jnp.sum(teacher_exp, axis=-1, keepdims=True)
    recv_label = jnp.where(recv_len > 0, recv_query, -1).astype(jnp.float32)
    shared = jnp.concatenate([slot_scores, recv_label, target.reshape(pairs)])
    table = lax.all_to_all(
        jnp.broadcast_to(shared[None], (devices, 2 * slots + pairs)),
        AXES,
        split_axis=0,
        concat_axis=0,
        tiled=True,
    )
    score_table = table[:, :slots]
    label_table = table[:, slots : 2 * slots]
    exp_table = jnp.exp(score_table)
    query_ids = jnp.arange(queries, dtype=jnp.float32)
    column_sums = jnp.sum(
        jnp.where(label_table[None] == query_ids[:, None, None], exp_table[None], 0.0), axis=1
    )
    column = jnp.arange(slots, dtype=jnp.int32)
    same_source = (column[:, None] // capacity == column[None, :] // capacity).astype(jnp.float32)
    source_sums = jnp.dot(column_sums, same_source, precision=lax.Precision.HIGHEST)
    student_sum = jnp.sum(
        jnp.where(
            recv_query[None, :] == jnp.arange(queries, dtype=jnp.int32)[:, None], source_sums, 0.0
        ),
        axis=0,
    )
    target_rows = jnp.repeat(table[:, 2 * slots :], capacity, axis=0)
    target_column = recv_query * candidates + recv_k
    slot_target = jnp.sum(
        jnp.where(
            jnp.arange(pairs, dtype=jnp.int32)[None, :] == target_column[:, None], target_rows, 0.0
        ),
        axis=1,
    )
    recv_weight = jnp.where(recv_len > 0, jnp.exp(slot_scores) / student_sum - slot_target, 0.0)

    me = lax.axis_index(AXES)
    mine = lax.dynamic_slice_in_dim(score_table, me * capacity, capacity, axis=1)
    flat_rank = rank_value
    owner_hit = flat_owner[:, None] == jnp.arange(devices, dtype=jnp.int32)[None, :]
    scores = jnp.zeros((pairs,), jnp.float32)
    for r in range(capacity):
        scores = scores + jnp.sum(
            jnp.where(owner_hit & (flat_rank[:, None] == r), mine[:, r][None, :], 0.0), axis=1
        )
    scores = scores.reshape(queries, candidates)
    _, divergence = distill(scores, teacher)

    query_part, passage_part = pair_grads(
        exponent_terms, exponent_total, recv_mask, recv_weight, recv_emb, passage_rows
    )
    passage_grad = jnp.einsum(
        "sp,sjd->jpd",
        passage_pick.astype(jnp.bfloat16),
        passage_part,
        preferred_element_type=jnp.float32,
    )
    returned_grads = exchange(query_part.reshape(slots, query_len * width), devices)
    query_grad = jnp.dot(
        query_pick.astype(jnp.bfloat16).T, returned_grads, preferred_element_type=jnp.float32
    ).reshape(queries, query_len, width)

    query_pre_grad = grad_pre_of(query_unit, query_norm, query_grad.reshape(queries * query_len, width))
    passage_pre_grad = grad_pre_of(
        passage_unit, passage_norm, passage_grad.reshape(passage_len * passages, width)
    )
    contract = (((0,), (0,)), ((), ()))
    local_grad = lax.dot_general(
        query_flat, query_pre_grad, contract, preferred_element_type=jnp.float32
    ) + lax.dot_general(passage_flat, passage_pre_grad, contract, preferred_element_type=jnp.float32)
    flat = jnp.concatenate([local_grad.reshape(-1), jnp.sum(divergence)[None]])
    total = all_sum(flat, devices)
    head_grad = total[: hidden * width].reshape(hidden, width)
    loss = total[hidden * width] / (queries * devices)
    return (scores, loss, head_grad)


def solution(mesh):
    return jax.shard_map(
        on_device,
        mesh=mesh,
        in_specs=(
            P(AXES, None, None),
            P(AXES, None, None),
            P(),
            P(AXES, None),
            P(AXES, None),
            P(AXES, None),
            P(AXES),
            P(AXES),
        ),
        out_specs=(P(AXES, None), P(), P()),
        check_vma=False,
    )
```

```python
import jax
import jax.numpy as jnp
from jax import lax
from jax.sharding import PartitionSpec as P

SOFTMAX_TEMP = 0.05
EPSILON = 1e-06
AXES = ("pb", "pa")
META = 128


def normalize(projected):
    norm_value = jnp.sqrt(jnp.sum(projected * projected, axis=-1, keepdims=True) + EPSILON)
    unit_rows = projected / norm_value
    return (unit_rows.astype(jnp.bfloat16), unit_rows, norm_value)


def grad_pre_of(unit_rows, norm_value, along):
    radial = jnp.sum(along * unit_rows, axis=-1, keepdims=True)
    return ((along - unit_rows * radial) / norm_value).astype(jnp.bfloat16)


def length_mask(lengths, width_value):
    return (jnp.arange(width_value, dtype=jnp.int32)[None, :] < lengths[:, None]).astype(
        jnp.float32
    )


def pair_terms(query_rows, passage_rows, passage_token_mask):
    token_similarity = jnp.einsum(
        "sid,sjd->sij", query_rows, passage_rows, preferred_element_type=jnp.float32
    )
    exponent_terms = jnp.exp(token_similarity / SOFTMAX_TEMP) * passage_token_mask[:, None, :]
    return (exponent_terms, jnp.sum(exponent_terms, axis=-1))


def pair_scores(exponent_total, query_token_mask):
    return jnp.sum(query_token_mask * (SOFTMAX_TEMP * jnp.log(exponent_total)), axis=-1)


def pair_grads(exponent_terms, exponent_total, query_token_mask, weights, query_rows, passage_rows):
    share = (
        (weights[:, None] * query_token_mask / exponent_total)[:, :, None] * exponent_terms
    ).astype(jnp.bfloat16)
    query_part = jnp.einsum(
        "sij,sjd->sid", share, passage_rows, preferred_element_type=jnp.float32
    ).astype(jnp.bfloat16)
    passage_part = jnp.einsum(
        "sij,sid->sjd", share, query_rows, preferred_element_type=jnp.float32
    ).astype(jnp.bfloat16)
    return (query_part, passage_part)


def distill(scores, teacher):
    student_exp = jnp.exp(scores)
    student_sum = jnp.sum(student_exp, axis=-1, keepdims=True)
    teacher_exp = jnp.exp(teacher)
    teacher_sum = jnp.sum(teacher_exp, axis=-1, keepdims=True)
    target = teacher_exp / teacher_sum
    divergence = jnp.sum(
        target * (teacher - jnp.log(teacher_sum) - (scores - jnp.log(student_sum))), axis=-1
    )
    return (student_exp / student_sum - target, divergence)


def exchange(values, devices):
    shaped = values.reshape((devices, -1) + values.shape[1:])
    moved = lax.all_to_all(shaped, AXES, split_axis=0, concat_axis=0, tiled=True)
    return moved.reshape(values.shape)


def all_sum(flat, devices):
    chunk = -(-flat.shape[0] // (devices * 128)) * 128
    padded = jnp.pad(flat, (0, devices * chunk - flat.shape[0]))
    gathered = lax.all_to_all(
        padded.reshape(devices, chunk), AXES, split_axis=0, concat_axis=0, tiled=True
    )
    reduced = jnp.sum(gathered, axis=0)
    spread = lax.all_to_all(
        jnp.broadcast_to(reduced[None], (devices, chunk)),
        AXES,
        split_axis=0,
        concat_axis=0,
        tiled=True,
    )
    return spread.reshape(-1)


def on_device(
    query_states,
    passage_states,
    head,
    teacher,
    cand_owner,
    cand_local,
    query_lengths,
    passage_lengths,
):
    devices = lax.axis_size("pb") * lax.axis_size("pa")
    queries, query_len, hidden = query_states.shape
    passages, passage_len, _ = passage_states.shape
    width = head.shape[1]
    candidates = cand_owner.shape[1]
    capacity = min(queries, max(2, 2 * queries * candidates // devices))
    slots = devices * capacity
    pairs = queries * candidates

    query_flat = query_states.reshape(queries * query_len, hidden)
    query_pre = jnp.dot(query_flat, head, preferred_element_type=jnp.float32)
    query_emb, query_unit, query_norm = normalize(query_pre)
    passage_flat = jnp.transpose(passage_states, (1, 0, 2)).reshape(passage_len * passages, hidden)
    passage_pre = jnp.dot(passage_flat, head, preferred_element_type=jnp.float32)
    passage_emb_flat, passage_unit, passage_norm = normalize(passage_pre)
    passage_emb = jnp.transpose(passage_emb_flat.reshape(passage_len, passages, width), (1, 0, 2))

    flat_owner = cand_owner.reshape(pairs)
    flat_local = cand_local.reshape(pairs)
    row_of = jnp.repeat(jnp.arange(queries, dtype=jnp.int32), candidates)
    k_of = jnp.tile(jnp.arange(candidates, dtype=jnp.int32), queries)
    same_owner = flat_owner[:, None] == flat_owner[None, :]
    earlier_row = row_of[None, :] < row_of[:, None]
    rank_value = jnp.sum((same_owner & earlier_row).astype(jnp.int32), axis=1)
    flat_slot = flat_owner * capacity + rank_value
    slot_pick = flat_slot[None, :] == jnp.arange(slots, dtype=jnp.int32)[:, None]
    slot_live = jnp.any(slot_pick, axis=1)
    slot_query = jnp.sum(jnp.where(slot_pick, row_of[None, :], 0), axis=1)
    slot_k = jnp.sum(jnp.where(slot_pick, k_of[None, :], 0), axis=1)
    slot_local = jnp.sum(jnp.where(slot_pick, flat_local[None, :], 0), axis=1)
    query_pick = (slot_query[:, None] == jnp.arange(queries, dtype=jnp.int32)[None, :]) & slot_live[
        :, None
    ]
    sent_len = jnp.sum(jnp.where(query_pick, query_lengths[None, :], 0), axis=1)
    sent_emb = jnp.einsum(
        "sq,qid->sid",
        query_pick.astype(jnp.bfloat16),
        query_emb.reshape(queries, query_len, width),
        preferred_element_type=jnp.float32,
    ).astype(jnp.bfloat16)
    lane = jnp.arange(width, dtype=jnp.int32)[None, :]
    meta = jnp.where(
        lane == 0,
        slot_local[:, None],
        jnp.where(
            lane == 1,
            sent_len[:, None],
            jnp.where(lane == 2, slot_query[:, None], jnp.where(lane == 3, slot_k[:, None], 0)),
        ),
    ).astype(jnp.bfloat16)
    emb_rows = capacity * query_len
    meta_rows = -(-capacity // 16) * 16
    meta_block = jnp.pad(
        meta.reshape(devices, capacity, width), ((0, 0), (0, meta_rows - capacity), (0, 0))
    )
    payload = jnp.concatenate([sent_emb.reshape(devices, emb_rows, width), meta_block], axis=1)
    got = lax.all_to_all(payload, AXES, split_axis=0, concat_axis=0, tiled=True)
    recv_emb = got[:, :emb_rows].reshape(slots, query_len, width)
    recv_meta = got[:, emb_rows : emb_rows + capacity, :4].reshape(slots, 4).astype(jnp.int32)
    recv_local = recv_meta[:, 0]
    recv_len = recv_meta[:, 1]
    recv_query = recv_meta[:, 2]
    recv_k = recv_meta[:, 3]
    recv_mask = length_mask(recv_len, query_len)

    passage_pick = recv_local[:, None] == jnp.arange(passages, dtype=jnp.int32)[None, :]
    passage_rows = jnp.einsum(
        "sp,pjd->sjd",
        passage_pick.astype(jnp.bfloat16),
        passage_emb,
        preferred_element_type=jnp.float32,
    ).astype(jnp.bfloat16)
    picked_len = jnp.sum(jnp.where(passage_pick, passage_lengths[None, :], 0), axis=1)
    passage_token_mask = length_mask(picked_len, passage_len)
    exponent_terms, exponent_total = pair_terms(recv_emb, passage_rows, passage_token_mask)
    slot_scores = pair_scores(exponent_total, recv_mask)

    teacher_exp = jnp.exp(teacher)
    target = teacher_exp / jnp.sum(teacher_exp, axis=-1, keepdims=True)
    recv_label = jnp.where(recv_len > 0, recv_query, -1).astype(jnp.float32)
    shared = jnp.concatenate([slot_scores, recv_label, target.reshape(pairs)])
    table = lax.all_to_all(
        jnp.broadcast_to(shared[None], (devices, 2 * slots + pairs)),
        AXES,
        split_axis=0,
        concat_axis=0,
        tiled=True,
    )
    score_table = table[:, :slots]
    label_table = table[:, slots : 2 * slots]
    exp_table = jnp.exp(score_table)
    query_ids = jnp.arange(queries, dtype=jnp.float32)
    column_sums = jnp.sum(
        jnp.where(label_table[None] == query_ids[:, None, None], exp_table[None], 0.0), axis=1
    )
    column = jnp.arange(slots, dtype=jnp.int32)
    same_source = (column[:, None] // capacity == column[None, :] // capacity).astype(jnp.float32)
    source_sums = jnp.dot(column_sums, same_source, precision=lax.Precision.HIGHEST)
    student_sum = jnp.sum(
        jnp.where(
            recv_query[None, :] == jnp.arange(queries, dtype=jnp.int32)[:, None], source_sums, 0.0
        ),
        axis=0,
    )
    target_rows = jnp.repeat(table[:, 2 * slots :], capacity, axis=0)
    target_column = recv_query * candidates + recv_k
    slot_target = jnp.sum(
        jnp.where(
            jnp.arange(pairs, dtype=jnp.int32)[None, :] == target_column[:, None], target_rows, 0.0
        ),
        axis=1,
    )
    recv_weight = jnp.where(recv_len > 0, jnp.exp(slot_scores) / student_sum - slot_target, 0.0)

    me = lax.axis_index(AXES)
    mine = lax.dynamic_slice_in_dim(score_table, me * capacity, capacity, axis=1)
    flat_rank = rank_value
    owner_hit = flat_owner[:, None] == jnp.arange(devices, dtype=jnp.int32)[None, :]
    scores = jnp.zeros((pairs,), jnp.float32)
    for r in range(capacity):
        scores = scores + jnp.sum(
            jnp.where(owner_hit & (flat_rank[:, None] == r), mine[:, r][None, :], 0.0), axis=1
        )
    scores = scores.reshape(queries, candidates)
    _, divergence = distill(scores, teacher)

    query_part, passage_part = pair_grads(
        exponent_terms, exponent_total, recv_mask, recv_weight, recv_emb, passage_rows
    )
    passage_grad = jnp.einsum(
        "sp,sjd->jpd",
        passage_pick.astype(jnp.bfloat16),
        passage_part,
        preferred_element_type=jnp.float32,
    )
    returned_grads = lax.all_to_all(
        query_part.reshape(devices, capacity * query_len, width),
        AXES,
        split_axis=0,
        concat_axis=0,
        tiled=True,
    ).reshape(slots, query_len, width)
    query_grad = jnp.einsum(
        "sq,sid->qid",
        query_pick.astype(jnp.bfloat16),
        returned_grads,
        preferred_element_type=jnp.float32,
    )

    query_pre_grad = grad_pre_of(query_unit, query_norm, query_grad.reshape(queries * query_len, width))
    passage_pre_grad = grad_pre_of(
        passage_unit, passage_norm, passage_grad.reshape(passage_len * passages, width)
    )
    contract = (((0,), (0,)), ((), ()))
    local_grad = lax.dot_general(
        query_flat, query_pre_grad, contract, preferred_element_type=jnp.float32
    ) + lax.dot_general(passage_flat, passage_pre_grad, contract, preferred_element_type=jnp.float32)
    flat = jnp.concatenate([local_grad.reshape(-1), jnp.sum(divergence)[None]])
    total = all_sum(flat, devices)
    head_grad = total[: hidden * width].reshape(hidden, width)
    loss = total[hidden * width] / (queries * devices)
    return (scores, loss, head_grad)


def solution(mesh):
    return jax.shard_map(
        on_device,
        mesh=mesh,
        in_specs=(
            P(AXES, None, None),
            P(AXES, None, None),
            P(),
            P(AXES, None),
            P(AXES, None),
            P(AXES, None),
            P(AXES),
            P(AXES),
        ),
        out_specs=(P(AXES, None), P(), P()),
        check_vma=False,
    )
```

```python
import jax
import jax.numpy as jnp
from jax import lax
from jax.sharding import PartitionSpec as P

SOFTMAX_TEMP = 0.05
EPSILON = 1e-06
AXES = ("pb", "pa")
META = 128


def normalize(projected):
    norm_value = jnp.sqrt(jnp.sum(projected * projected, axis=-1, keepdims=True) + EPSILON)
    unit_rows = projected / norm_value
    return (unit_rows.astype(jnp.bfloat16), unit_rows, norm_value)


def grad_pre_of(unit_rows, norm_value, along):
    radial = jnp.sum(along * unit_rows, axis=-1, keepdims=True)
    return ((along - unit_rows * radial) / norm_value).astype(jnp.bfloat16)


def length_mask(lengths, width_value):
    return (jnp.arange(width_value, dtype=jnp.int32)[None, :] < lengths[:, None]).astype(
        jnp.float32
    )


def pair_terms(query_rows, passage_rows, passage_token_mask):
    token_similarity = jnp.einsum(
        "sid,sjd->sij", query_rows, passage_rows, preferred_element_type=jnp.float32
    )
    exponent_terms = jnp.exp(token_similarity / SOFTMAX_TEMP) * passage_token_mask[:, None, :]
    return (exponent_terms, jnp.sum(exponent_terms, axis=-1))


def pair_scores(exponent_total, query_token_mask):
    return jnp.sum(query_token_mask * (SOFTMAX_TEMP * jnp.log(exponent_total)), axis=-1)


def pair_grads(exponent_terms, exponent_total, query_token_mask, weights, query_rows, passage_rows):
    share = (
        (weights[:, None] * query_token_mask / exponent_total)[:, :, None] * exponent_terms
    ).astype(jnp.bfloat16)
    query_part = jnp.einsum(
        "sij,sjd->sid", share, passage_rows, preferred_element_type=jnp.float32
    ).astype(jnp.bfloat16)
    passage_part = jnp.einsum(
        "sij,sid->sjd", share, query_rows, preferred_element_type=jnp.float32
    ).astype(jnp.bfloat16)
    return (query_part, passage_part)


def distill(scores, teacher):
    student_exp = jnp.exp(scores)
    student_sum = jnp.sum(student_exp, axis=-1, keepdims=True)
    teacher_exp = jnp.exp(teacher)
    teacher_sum = jnp.sum(teacher_exp, axis=-1, keepdims=True)
    target = teacher_exp / teacher_sum
    divergence = jnp.sum(
        target * (teacher - jnp.log(teacher_sum) - (scores - jnp.log(student_sum))), axis=-1
    )
    return (student_exp / student_sum - target, divergence)


def exchange(values, devices):
    shaped = values.reshape((devices, -1) + values.shape[1:])
    moved = lax.all_to_all(shaped, AXES, split_axis=0, concat_axis=0, tiled=True)
    return moved.reshape(values.shape)


def all_sum(flat, devices):
    chunk = -(-flat.shape[0] // (devices * 128)) * 128
    padded = jnp.pad(flat, (0, devices * chunk - flat.shape[0]))
    gathered = lax.all_to_all(
        padded.reshape(devices, chunk), AXES, split_axis=0, concat_axis=0, tiled=True
    )
    reduced = jnp.sum(gathered, axis=0)
    spread = lax.all_to_all(
        jnp.broadcast_to(reduced[None], (devices, chunk)),
        AXES,
        split_axis=0,
        concat_axis=0,
        tiled=True,
    )
    return spread.reshape(-1)


def on_device(
    query_states,
    passage_states,
    head,
    teacher,
    cand_owner,
    cand_local,
    query_lengths,
    passage_lengths,
):
    devices = lax.axis_size("pb") * lax.axis_size("pa")
    queries, query_len, hidden = query_states.shape
    passages, passage_len, _ = passage_states.shape
    width = head.shape[1]
    candidates = cand_owner.shape[1]
    capacity = min(queries, max(2, 2 * queries * candidates // devices))
    slots = devices * capacity
    pairs = queries * candidates

    query_flat = query_states.reshape(queries * query_len, hidden)
    query_pre = jnp.dot(query_flat, head, preferred_element_type=jnp.float32)
    query_emb, query_unit, query_norm = normalize(query_pre)
    passage_flat = jnp.transpose(passage_states, (1, 0, 2)).reshape(passage_len * passages, hidden)
    passage_pre = jnp.dot(passage_flat, head, preferred_element_type=jnp.float32)
    passage_emb_flat, passage_unit, passage_norm = normalize(passage_pre)
    passage_emb = jnp.transpose(passage_emb_flat.reshape(passage_len, passages, width), (1, 0, 2))

    flat_owner = cand_owner.reshape(pairs)
    flat_local = cand_local.reshape(pairs)
    row_of = jnp.repeat(jnp.arange(queries, dtype=jnp.int32), candidates)
    k_of = jnp.tile(jnp.arange(candidates, dtype=jnp.int32), queries)
    same_owner = flat_owner[:, None] == flat_owner[None, :]
    earlier_row = row_of[None, :] < row_of[:, None]
    rank_value = jnp.sum((same_owner & earlier_row).astype(jnp.int32), axis=1)
    flat_slot = flat_owner * capacity + rank_value
    slot_pick = flat_slot[None, :] == jnp.arange(slots, dtype=jnp.int32)[:, None]
    slot_live = jnp.any(slot_pick, axis=1)
    slot_query = jnp.sum(jnp.where(slot_pick, row_of[None, :], 0), axis=1)
    slot_k = jnp.sum(jnp.where(slot_pick, k_of[None, :], 0), axis=1)
    slot_local = jnp.sum(jnp.where(slot_pick, flat_local[None, :], 0), axis=1)
    query_pick = (slot_query[:, None] == jnp.arange(queries, dtype=jnp.int32)[None, :]) & slot_live[
        :, None
    ]
    sent_len = jnp.sum(jnp.where(query_pick, query_lengths[None, :], 0), axis=1)
    sent_emb = jnp.einsum(
        "sq,qid->sid",
        query_pick.astype(jnp.bfloat16),
        query_emb.reshape(queries, query_len, width),
        preferred_element_type=jnp.float32,
    ).astype(jnp.bfloat16)
    lane = jnp.arange(width, dtype=jnp.int32)[None, :]
    meta = jnp.where(
        lane == 0,
        slot_local[:, None],
        jnp.where(
            lane == 1,
            sent_len[:, None],
            jnp.where(lane == 2, slot_query[:, None], jnp.where(lane == 3, slot_k[:, None], 0)),
        ),
    ).astype(jnp.bfloat16)
    emb_rows = capacity * query_len
    meta_rows = -(-capacity // 16) * 16
    meta_block = jnp.pad(
        meta.reshape(devices, capacity, width), ((0, 0), (0, meta_rows - capacity), (0, 0))
    )
    payload = jnp.concatenate([sent_emb.reshape(devices, emb_rows, width), meta_block], axis=1)
    got = lax.all_to_all(payload, AXES, split_axis=0, concat_axis=0, tiled=True)
    recv_emb = got[:, :emb_rows].reshape(slots, query_len, width)
    recv_meta = got[:, emb_rows : emb_rows + capacity, :4].reshape(slots, 4).astype(jnp.int32)
    recv_local = recv_meta[:, 0]
    recv_len = recv_meta[:, 1]
    recv_query = recv_meta[:, 2]
    recv_k = recv_meta[:, 3]
    recv_mask = length_mask(recv_len, query_len)

    passage_pick = recv_local[:, None] == jnp.arange(passages, dtype=jnp.int32)[None, :]
    passage_rows = jnp.einsum(
        "sp,pjd->sjd",
        passage_pick.astype(jnp.bfloat16),
        passage_emb,
        preferred_element_type=jnp.float32,
    ).astype(jnp.bfloat16)
    picked_len = jnp.sum(jnp.where(passage_pick, passage_lengths[None, :], 0), axis=1)
    passage_token_mask = length_mask(picked_len, passage_len)
    exponent_terms, exponent_total = pair_terms(recv_emb, passage_rows, passage_token_mask)
    slot_scores = pair_scores(exponent_total, recv_mask)

    teacher_exp = jnp.exp(teacher)
    target = teacher_exp / jnp.sum(teacher_exp, axis=-1, keepdims=True)
    recv_label = jnp.where(recv_len > 0, recv_query, -1).astype(jnp.float32)
    shared = jnp.concatenate([slot_scores, recv_label, target.reshape(pairs)])
    table = lax.all_to_all(
        jnp.broadcast_to(shared[None], (devices, 2 * slots + pairs)),
        AXES,
        split_axis=0,
        concat_axis=0,
        tiled=True,
    )
    score_table = table[:, :slots]
    label_table = table[:, slots : 2 * slots]
    exp_table = jnp.exp(score_table)
    query_ids = jnp.arange(queries, dtype=jnp.float32)
    column_sums = jnp.sum(
        jnp.where(label_table[None] == query_ids[:, None, None], exp_table[None], 0.0), axis=1
    )
    column = jnp.arange(slots, dtype=jnp.int32)
    same_source = (column[:, None] // capacity == column[None, :] // capacity).astype(jnp.float32)
    source_sums = jnp.dot(column_sums, same_source, precision=lax.Precision.HIGHEST)
    student_sum = jnp.sum(
        jnp.where(
            recv_query[None, :] == jnp.arange(queries, dtype=jnp.int32)[:, None], source_sums, 0.0
        ),
        axis=0,
    )
    target_rows = jnp.repeat(table[:, 2 * slots :], capacity, axis=0)
    target_column = recv_query * candidates + recv_k
    slot_target = jnp.sum(
        jnp.where(
            jnp.arange(pairs, dtype=jnp.int32)[None, :] == target_column[:, None], target_rows, 0.0
        ),
        axis=1,
    )
    recv_weight = jnp.where(recv_len > 0, jnp.exp(slot_scores) / student_sum - slot_target, 0.0)

    me = lax.axis_index(AXES)
    mine = lax.dynamic_slice_in_dim(score_table, me * capacity, capacity, axis=1)
    flat_rank = rank_value
    owner_hit = flat_owner[:, None] == jnp.arange(devices, dtype=jnp.int32)[None, :]
    scores = jnp.zeros((pairs,), jnp.float32)
    for r in range(capacity):
        scores = scores + jnp.sum(
            jnp.where(owner_hit & (flat_rank[:, None] == r), mine[:, r][None, :], 0.0), axis=1
        )
    scores = scores.reshape(queries, candidates)
    _, divergence = distill(scores, teacher)

    share = (
        (recv_weight[:, None] * recv_mask / exponent_total)[:, :, None] * exponent_terms
    ).astype(jnp.bfloat16)
    query_part = jnp.einsum(
        "sij,sjd->sid", share, passage_rows, preferred_element_type=jnp.float32
    ).astype(jnp.bfloat16)
    returned_grads = lax.all_to_all(
        query_part.reshape(devices, capacity * query_len, width),
        AXES,
        split_axis=0,
        concat_axis=0,
        tiled=True,
    ).reshape(slots, query_len, width)
    share, recv_rows = lax.optimization_barrier((share, recv_emb))
    passage_part = jnp.einsum(
        "sij,sid->sjd", share, recv_rows, preferred_element_type=jnp.float32
    ).astype(jnp.bfloat16)
    passage_grad = jnp.einsum(
        "sp,sjd->jpd",
        passage_pick.astype(jnp.bfloat16),
        passage_part,
        preferred_element_type=jnp.float32,
    )
    query_grad = jnp.einsum(
        "sq,sid->qid",
        query_pick.astype(jnp.bfloat16),
        returned_grads,
        preferred_element_type=jnp.float32,
    )

    query_pre_grad = grad_pre_of(query_unit, query_norm, query_grad.reshape(queries * query_len, width))
    passage_pre_grad = grad_pre_of(
        passage_unit, passage_norm, passage_grad.reshape(passage_len * passages, width)
    )
    contract = (((0,), (0,)), ((), ()))
    local_grad = lax.dot_general(
        query_flat, query_pre_grad, contract, preferred_element_type=jnp.float32
    ) + lax.dot_general(passage_flat, passage_pre_grad, contract, preferred_element_type=jnp.float32)
    flat = jnp.concatenate([local_grad.reshape(-1), jnp.sum(divergence)[None]])
    total = all_sum(flat, devices)
    head_grad = total[: hidden * width].reshape(hidden, width)
    loss = total[hidden * width] / (queries * devices)
    return (scores, loss, head_grad)


def solution(mesh):
    return jax.shard_map(
        on_device,
        mesh=mesh,
        in_specs=(
            P(AXES, None, None),
            P(AXES, None, None),
            P(),
            P(AXES, None),
            P(AXES, None),
            P(AXES, None),
            P(AXES),
            P(AXES),
        ),
        out_specs=(P(AXES, None), P(), P()),
        check_vma=False,
    )
```

```python
import jax
import jax.numpy as jnp
from jax import lax
from jax.sharding import PartitionSpec as P

SOFTMAX_TEMP = 0.05
EPSILON = 1e-06
AXES = ("pb", "pa")
META = 128


def normalize(projected):
    norm_value = jnp.sqrt(jnp.sum(projected * projected, axis=-1, keepdims=True) + EPSILON)
    unit_rows = projected / norm_value
    return (unit_rows.astype(jnp.bfloat16), unit_rows, norm_value)


def grad_pre_of(unit_rows, norm_value, along):
    radial = jnp.sum(along * unit_rows, axis=-1, keepdims=True)
    return ((along - unit_rows * radial) / norm_value).astype(jnp.bfloat16)


def length_mask(lengths, width_value):
    return (jnp.arange(width_value, dtype=jnp.int32)[None, :] < lengths[:, None]).astype(
        jnp.float32
    )


def pair_terms(query_rows, passage_rows, passage_token_mask):
    token_similarity = jnp.einsum(
        "sid,sjd->sij", query_rows, passage_rows, preferred_element_type=jnp.float32
    )
    exponent_terms = jnp.exp(token_similarity / SOFTMAX_TEMP) * passage_token_mask[:, None, :]
    return (exponent_terms, jnp.sum(exponent_terms, axis=-1))


def pair_scores(exponent_total, query_token_mask):
    return jnp.sum(query_token_mask * (SOFTMAX_TEMP * jnp.log(exponent_total)), axis=-1)


def pair_grads(exponent_terms, exponent_total, query_token_mask, weights, query_rows, passage_rows):
    share = (
        (weights[:, None] * query_token_mask / exponent_total)[:, :, None] * exponent_terms
    ).astype(jnp.bfloat16)
    query_part = jnp.einsum(
        "sij,sjd->sid", share, passage_rows, preferred_element_type=jnp.float32
    ).astype(jnp.bfloat16)
    passage_part = jnp.einsum(
        "sij,sid->sjd", share, query_rows, preferred_element_type=jnp.float32
    ).astype(jnp.bfloat16)
    return (query_part, passage_part)


def distill(scores, teacher):
    student_exp = jnp.exp(scores)
    student_sum = jnp.sum(student_exp, axis=-1, keepdims=True)
    teacher_exp = jnp.exp(teacher)
    teacher_sum = jnp.sum(teacher_exp, axis=-1, keepdims=True)
    target = teacher_exp / teacher_sum
    divergence = jnp.sum(
        target * (teacher - jnp.log(teacher_sum) - (scores - jnp.log(student_sum))), axis=-1
    )
    return (student_exp / student_sum - target, divergence)


def exchange(values, devices):
    shaped = values.reshape((devices, -1) + values.shape[1:])
    moved = lax.all_to_all(shaped, AXES, split_axis=0, concat_axis=0, tiled=True)
    return moved.reshape(values.shape)


def all_sum(flat, devices):
    chunk = -(-flat.shape[0] // (devices * 128)) * 128
    padded = jnp.pad(flat, (0, devices * chunk - flat.shape[0]))
    gathered = lax.all_to_all(
        padded.reshape(devices, chunk), AXES, split_axis=0, concat_axis=0, tiled=True
    )
    reduced = jnp.sum(gathered, axis=0)
    spread = lax.all_to_all(
        jnp.broadcast_to(reduced[None], (devices, chunk)),
        AXES,
        split_axis=0,
        concat_axis=0,
        tiled=True,
    )
    return spread.reshape(-1)


def on_device(
    query_states,
    passage_states,
    head,
    teacher,
    cand_owner,
    cand_local,
    query_lengths,
    passage_lengths,
):
    devices = lax.axis_size("pb") * lax.axis_size("pa")
    queries, query_len, hidden = query_states.shape
    passages, passage_len, _ = passage_states.shape
    width = head.shape[1]
    candidates = cand_owner.shape[1]
    capacity = min(queries, max(2, 2 * queries * candidates // devices))
    slots = devices * capacity
    pairs = queries * candidates

    query_flat = query_states.reshape(queries * query_len, hidden)
    query_pre = jnp.dot(query_flat, head, preferred_element_type=jnp.float32)
    query_emb, query_unit, query_norm = normalize(query_pre)
    passage_flat = jnp.transpose(passage_states, (1, 0, 2)).reshape(passage_len * passages, hidden)
    passage_pre = jnp.dot(passage_flat, head, preferred_element_type=jnp.float32)
    passage_emb_flat, passage_unit, passage_norm = normalize(passage_pre)
    passage_emb = jnp.transpose(passage_emb_flat.reshape(passage_len, passages, width), (1, 0, 2))

    flat_owner = cand_owner.reshape(pairs)
    flat_local = cand_local.reshape(pairs)
    row_of = jnp.repeat(jnp.arange(queries, dtype=jnp.int32), candidates)
    k_of = jnp.tile(jnp.arange(candidates, dtype=jnp.int32), queries)
    same_owner = flat_owner[:, None] == flat_owner[None, :]
    earlier_row = row_of[None, :] < row_of[:, None]
    rank_value = jnp.sum((same_owner & earlier_row).astype(jnp.int32), axis=1)
    flat_slot = flat_owner * capacity + rank_value
    slot_pick = flat_slot[None, :] == jnp.arange(slots, dtype=jnp.int32)[:, None]
    slot_live = jnp.any(slot_pick, axis=1)
    slot_query = jnp.sum(jnp.where(slot_pick, row_of[None, :], 0), axis=1)
    slot_k = jnp.sum(jnp.where(slot_pick, k_of[None, :], 0), axis=1)
    slot_local = jnp.sum(jnp.where(slot_pick, flat_local[None, :], 0), axis=1)
    query_pick = (slot_query[:, None] == jnp.arange(queries, dtype=jnp.int32)[None, :]) & slot_live[
        :, None
    ]
    sent_len = jnp.sum(jnp.where(query_pick, query_lengths[None, :], 0), axis=1)
    lane = jnp.arange(width, dtype=jnp.int32)[None, :]
    meta = jnp.where(
        lane == 0,
        slot_local[:, None],
        jnp.where(
            lane == 1,
            sent_len[:, None],
            jnp.where(lane == 2, slot_query[:, None], jnp.where(lane == 3, slot_k[:, None], 0)),
        ),
    ).astype(jnp.bfloat16)
    emb_rows = capacity * query_len
    meta_rows = -(-capacity // 16) * 16
    sources = jnp.concatenate([query_emb.reshape(queries * query_len, width), meta], axis=0)
    token = jnp.arange(emb_rows, dtype=jnp.int32)[None, :] % query_len
    emb_source = jnp.repeat(slot_query.reshape(devices, capacity), query_len, axis=1) * query_len + token
    emb_source = jnp.where(
        jnp.repeat(slot_live.reshape(devices, capacity), query_len, axis=1), emb_source, -1
    )
    extra = jnp.arange(meta_rows, dtype=jnp.int32)[None, :]
    meta_source = jnp.where(
        extra < capacity,
        queries * query_len + jnp.arange(devices, dtype=jnp.int32)[:, None] * capacity + extra,
        -1,
    )
    source_row = jnp.concatenate([emb_source, meta_source], axis=1)
    pick = (
        source_row[:, :, None]
        == jnp.arange(queries * query_len + slots, dtype=jnp.int32)[None, None, :]
    ).astype(jnp.bfloat16)
    payload = (
        jnp.dot(
            pick.reshape(devices * (emb_rows + meta_rows), -1),
            sources,
            preferred_element_type=jnp.float32,
        )
        .astype(jnp.bfloat16)
        .reshape(devices, emb_rows + meta_rows, width)
    )
    got = lax.all_to_all(payload, AXES, split_axis=0, concat_axis=0, tiled=True)
    recv_emb = got[:, :emb_rows].reshape(slots, query_len, width)
    recv_meta = got[:, emb_rows : emb_rows + capacity, :4].reshape(slots, 4).astype(jnp.int32)
    recv_local = recv_meta[:, 0]
    recv_len = recv_meta[:, 1]
    recv_query = recv_meta[:, 2]
    recv_k = recv_meta[:, 3]
    recv_mask = length_mask(recv_len, query_len)

    passage_pick = recv_local[:, None] == jnp.arange(passages, dtype=jnp.int32)[None, :]
    passage_rows = jnp.einsum(
        "sp,pjd->sjd",
        passage_pick.astype(jnp.bfloat16),
        passage_emb,
        preferred_element_type=jnp.float32,
    ).astype(jnp.bfloat16)
    picked_len = jnp.sum(jnp.where(passage_pick, passage_lengths[None, :], 0), axis=1)
    passage_token_mask = length_mask(picked_len, passage_len)
    exponent_terms, exponent_total = pair_terms(recv_emb, passage_rows, passage_token_mask)
    slot_scores = pair_scores(exponent_total, recv_mask)

    teacher_exp = jnp.exp(teacher)
    target = teacher_exp / jnp.sum(teacher_exp, axis=-1, keepdims=True)
    recv_label = jnp.where(recv_len > 0, recv_query, -1).astype(jnp.float32)
    shared = jnp.concatenate([slot_scores, recv_label, target.reshape(pairs)])
    table = lax.all_to_all(
        jnp.broadcast_to(shared[None], (devices, 2 * slots + pairs)),
        AXES,
        split_axis=0,
        concat_axis=0,
        tiled=True,
    )
    score_table = table[:, :slots]
    label_table = table[:, slots : 2 * slots]
    exp_table = jnp.exp(score_table)
    query_ids = jnp.arange(queries, dtype=jnp.float32)
    column_sums = jnp.sum(
        jnp.where(label_table[None] == query_ids[:, None, None], exp_table[None], 0.0), axis=1
    )
    column = jnp.arange(slots, dtype=jnp.int32)
    same_source = (column[:, None] // capacity == column[None, :] // capacity).astype(jnp.float32)
    source_sums = jnp.dot(column_sums, same_source, precision=lax.Precision.HIGHEST)
    student_sum = jnp.sum(
        jnp.where(
            recv_query[None, :] == jnp.arange(queries, dtype=jnp.int32)[:, None], source_sums, 0.0
        ),
        axis=0,
    )
    target_rows = jnp.repeat(table[:, 2 * slots :], capacity, axis=0)
    target_column = recv_query * candidates + recv_k
    slot_target = jnp.sum(
        jnp.where(
            jnp.arange(pairs, dtype=jnp.int32)[None, :] == target_column[:, None], target_rows, 0.0
        ),
        axis=1,
    )
    recv_weight = jnp.where(recv_len > 0, jnp.exp(slot_scores) / student_sum - slot_target, 0.0)

    me = lax.axis_index(AXES)
    mine = lax.dynamic_slice_in_dim(score_table, me * capacity, capacity, axis=1)
    flat_rank = rank_value
    owner_hit = flat_owner[:, None] == jnp.arange(devices, dtype=jnp.int32)[None, :]
    scores = jnp.zeros((pairs,), jnp.float32)
    for r in range(capacity):
        scores = scores + jnp.sum(
            jnp.where(owner_hit & (flat_rank[:, None] == r), mine[:, r][None, :], 0.0), axis=1
        )
    scores = scores.reshape(queries, candidates)
    _, divergence = distill(scores, teacher)

    query_part, passage_part = pair_grads(
        exponent_terms, exponent_total, recv_mask, recv_weight, recv_emb, passage_rows
    )
    passage_grad = jnp.einsum(
        "sp,sjd->jpd",
        passage_pick.astype(jnp.bfloat16),
        passage_part,
        preferred_element_type=jnp.float32,
    )
    returned_grads = lax.all_to_all(
        query_part.reshape(devices, capacity * query_len, width),
        AXES,
        split_axis=0,
        concat_axis=0,
        tiled=True,
    ).reshape(slots, query_len, width)
    query_grad = jnp.einsum(
        "sq,sid->qid",
        query_pick.astype(jnp.bfloat16),
        returned_grads,
        preferred_element_type=jnp.float32,
    )

    query_pre_grad = grad_pre_of(query_unit, query_norm, query_grad.reshape(queries * query_len, width))
    passage_pre_grad = grad_pre_of(
        passage_unit, passage_norm, passage_grad.reshape(passage_len * passages, width)
    )
    contract = (((0,), (0,)), ((), ()))
    local_grad = lax.dot_general(
        query_flat, query_pre_grad, contract, preferred_element_type=jnp.float32
    ) + lax.dot_general(passage_flat, passage_pre_grad, contract, preferred_element_type=jnp.float32)
    flat = jnp.concatenate([local_grad.reshape(-1), jnp.sum(divergence)[None]])
    total = all_sum(flat, devices)
    head_grad = total[: hidden * width].reshape(hidden, width)
    loss = total[hidden * width] / (queries * devices)
    return (scores, loss, head_grad)


def solution(mesh):
    return jax.shard_map(
        on_device,
        mesh=mesh,
        in_specs=(
            P(AXES, None, None),
            P(AXES, None, None),
            P(),
            P(AXES, None),
            P(AXES, None),
            P(AXES, None),
            P(AXES),
            P(AXES),
        ),
        out_specs=(P(AXES, None), P(), P()),
        check_vma=False,
    )
```

```python
import jax
import jax.numpy as jnp
from jax import lax
from jax.sharding import PartitionSpec as P

SOFTMAX_TEMP = 0.05
EPSILON = 1e-06
AXES = ("pb", "pa")
META = 128


def normalize(projected):
    norm_value = jnp.sqrt(jnp.sum(projected * projected, axis=-1, keepdims=True) + EPSILON)
    unit_rows = projected / norm_value
    return (unit_rows.astype(jnp.bfloat16), unit_rows, norm_value)


def grad_pre_of(unit_rows, norm_value, along):
    radial = jnp.sum(along * unit_rows, axis=-1, keepdims=True)
    return ((along - unit_rows * radial) / norm_value).astype(jnp.bfloat16)


def length_mask(lengths, width_value):
    return (jnp.arange(width_value, dtype=jnp.int32)[None, :] < lengths[:, None]).astype(
        jnp.float32
    )


def pair_terms(query_rows, passage_rows, passage_token_mask):
    token_similarity = jnp.einsum(
        "sid,sjd->sij", query_rows, passage_rows, preferred_element_type=jnp.float32
    )
    exponent_terms = jnp.exp(token_similarity / SOFTMAX_TEMP) * passage_token_mask[:, None, :]
    return (exponent_terms, jnp.sum(exponent_terms, axis=-1))


def pair_scores(exponent_total, query_token_mask):
    return jnp.sum(query_token_mask * (SOFTMAX_TEMP * jnp.log(exponent_total)), axis=-1)


def pair_grads(exponent_terms, exponent_total, query_token_mask, weights, query_rows, passage_rows):
    share = (
        (weights[:, None] * query_token_mask / exponent_total)[:, :, None] * exponent_terms
    ).astype(jnp.bfloat16)
    query_part = jnp.einsum(
        "sij,sjd->sid", share, passage_rows, preferred_element_type=jnp.float32
    ).astype(jnp.bfloat16)
    passage_part = jnp.einsum(
        "sij,sid->sjd", share, query_rows, preferred_element_type=jnp.float32
    ).astype(jnp.bfloat16)
    return (query_part, passage_part)


def distill(scores, teacher):
    student_exp = jnp.exp(scores)
    student_sum = jnp.sum(student_exp, axis=-1, keepdims=True)
    teacher_exp = jnp.exp(teacher)
    teacher_sum = jnp.sum(teacher_exp, axis=-1, keepdims=True)
    target = teacher_exp / teacher_sum
    divergence = jnp.sum(
        target * (teacher - jnp.log(teacher_sum) - (scores - jnp.log(student_sum))), axis=-1
    )
    return (student_exp / student_sum - target, divergence)


def exchange(values, devices):
    shaped = values.reshape((devices, -1) + values.shape[1:])
    moved = lax.all_to_all(shaped, AXES, split_axis=0, concat_axis=0, tiled=True)
    return moved.reshape(values.shape)


def all_sum(flat, devices):
    chunk = -(-flat.shape[0] // (devices * 128)) * 128
    padded = jnp.pad(flat, (0, devices * chunk - flat.shape[0]))
    gathered = lax.all_to_all(
        padded.reshape(devices, chunk), AXES, split_axis=0, concat_axis=0, tiled=True
    )
    reduced = jnp.sum(gathered, axis=0)
    spread = lax.all_to_all(
        jnp.broadcast_to(reduced[None], (devices, chunk)),
        AXES,
        split_axis=0,
        concat_axis=0,
        tiled=True,
    )
    return spread.reshape(-1)


def on_device(
    query_states,
    passage_states,
    head,
    teacher,
    cand_owner,
    cand_local,
    query_lengths,
    passage_lengths,
):
    devices = lax.axis_size("pb") * lax.axis_size("pa")
    queries, query_len, hidden = query_states.shape
    passages, passage_len, _ = passage_states.shape
    width = head.shape[1]
    candidates = cand_owner.shape[1]
    capacity = min(queries, max(2, 2 * queries * candidates // devices))
    slots = devices * capacity
    pairs = queries * candidates

    query_flat = query_states.reshape(queries * query_len, hidden)
    query_pre = jnp.dot(query_flat, head, preferred_element_type=jnp.float32)
    query_emb, query_unit, query_norm = normalize(query_pre)
    passage_flat = jnp.transpose(passage_states, (1, 0, 2)).reshape(passage_len * passages, hidden)
    passage_pre = jnp.dot(passage_flat, head, preferred_element_type=jnp.float32)
    passage_emb_flat, passage_unit, passage_norm = normalize(passage_pre)
    passage_emb = jnp.transpose(passage_emb_flat.reshape(passage_len, passages, width), (1, 0, 2))

    flat_owner = cand_owner.reshape(pairs)
    flat_local = cand_local.reshape(pairs)
    row_of = jnp.repeat(jnp.arange(queries, dtype=jnp.int32), candidates)
    k_of = jnp.tile(jnp.arange(candidates, dtype=jnp.int32), queries)
    same_owner = flat_owner[:, None] == flat_owner[None, :]
    earlier_row = row_of[None, :] < row_of[:, None]
    rank_value = jnp.sum((same_owner & earlier_row).astype(jnp.int32), axis=1)
    flat_slot = flat_owner * capacity + rank_value
    slot_pick = flat_slot[None, :] == jnp.arange(slots, dtype=jnp.int32)[:, None]
    slot_live = jnp.any(slot_pick, axis=1)
    slot_query = jnp.sum(jnp.where(slot_pick, row_of[None, :], 0), axis=1)
    slot_k = jnp.sum(jnp.where(slot_pick, k_of[None, :], 0), axis=1)
    slot_local = jnp.sum(jnp.where(slot_pick, flat_local[None, :], 0), axis=1)
    query_pick = (slot_query[:, None] == jnp.arange(queries, dtype=jnp.int32)[None, :]) & slot_live[
        :, None
    ]
    sent_len = jnp.sum(jnp.where(query_pick, query_lengths[None, :], 0), axis=1)
    sent_emb = jnp.sum(
        jnp.where(
            query_pick[:, :, None, None],
            query_emb.reshape(queries, query_len, width)[None].astype(jnp.float32),
            0.0,
        ),
        axis=1,
    ).astype(jnp.bfloat16)
    lane = jnp.arange(width, dtype=jnp.int32)[None, :]
    meta = jnp.where(
        lane == 0,
        slot_local[:, None],
        jnp.where(
            lane == 1,
            sent_len[:, None],
            jnp.where(lane == 2, slot_query[:, None], jnp.where(lane == 3, slot_k[:, None], 0)),
        ),
    ).astype(jnp.bfloat16)
    emb_rows = capacity * query_len
    meta_rows = -(-capacity // 16) * 16
    meta_block = jnp.pad(
        meta.reshape(devices, capacity, width), ((0, 0), (emb_rows, meta_rows - capacity), (0, 0))
    )
    payload = (
        jnp.pad(sent_emb.reshape(devices, emb_rows, width), ((0, 0), (0, meta_rows), (0, 0)))
        + meta_block
    )
    got = lax.all_to_all(payload, AXES, split_axis=0, concat_axis=0, tiled=True)
    recv_emb = got[:, :emb_rows].reshape(slots, query_len, width)
    recv_meta = got[:, emb_rows : emb_rows + capacity, :4].reshape(slots, 4).astype(jnp.int32)
    recv_local = recv_meta[:, 0]
    recv_len = recv_meta[:, 1]
    recv_query = recv_meta[:, 2]
    recv_k = recv_meta[:, 3]
    recv_mask = length_mask(recv_len, query_len)

    passage_pick = recv_local[:, None] == jnp.arange(passages, dtype=jnp.int32)[None, :]
    passage_rows = jnp.einsum(
        "sp,pjd->sjd",
        passage_pick.astype(jnp.bfloat16),
        passage_emb,
        preferred_element_type=jnp.float32,
    ).astype(jnp.bfloat16)
    picked_len = jnp.sum(jnp.where(passage_pick, passage_lengths[None, :], 0), axis=1)
    passage_token_mask = length_mask(picked_len, passage_len)
    exponent_terms, exponent_total = pair_terms(recv_emb, passage_rows, passage_token_mask)
    slot_scores = pair_scores(exponent_total, recv_mask)

    teacher_exp = jnp.exp(teacher)
    target = teacher_exp / jnp.sum(teacher_exp, axis=-1, keepdims=True)
    recv_label = jnp.where(recv_len > 0, recv_query, -1).astype(jnp.float32)
    shared = jnp.concatenate([slot_scores, recv_label, target.reshape(pairs)])
    table = lax.all_to_all(
        jnp.broadcast_to(shared[None], (devices, 2 * slots + pairs)),
        AXES,
        split_axis=0,
        concat_axis=0,
        tiled=True,
    )
    score_table = table[:, :slots]
    label_table = table[:, slots : 2 * slots]
    exp_table = jnp.exp(score_table)
    query_ids = jnp.arange(queries, dtype=jnp.float32)
    column_sums = jnp.sum(
        jnp.where(label_table[None] == query_ids[:, None, None], exp_table[None], 0.0), axis=1
    )
    column = jnp.arange(slots, dtype=jnp.int32)
    same_source = (column[:, None] // capacity == column[None, :] // capacity).astype(jnp.float32)
    source_sums = jnp.dot(column_sums, same_source, precision=lax.Precision.HIGHEST)
    student_sum = jnp.sum(
        jnp.where(
            recv_query[None, :] == jnp.arange(queries, dtype=jnp.int32)[:, None], source_sums, 0.0
        ),
        axis=0,
    )
    target_rows = jnp.repeat(table[:, 2 * slots :], capacity, axis=0)
    target_column = recv_query * candidates + recv_k
    slot_target = jnp.sum(
        jnp.where(
            jnp.arange(pairs, dtype=jnp.int32)[None, :] == target_column[:, None], target_rows, 0.0
        ),
        axis=1,
    )
    recv_weight = jnp.where(recv_len > 0, jnp.exp(slot_scores) / student_sum - slot_target, 0.0)

    me = lax.axis_index(AXES)
    mine = lax.dynamic_slice_in_dim(score_table, me * capacity, capacity, axis=1)
    flat_rank = rank_value
    owner_hit = flat_owner[:, None] == jnp.arange(devices, dtype=jnp.int32)[None, :]
    scores = jnp.zeros((pairs,), jnp.float32)
    for r in range(capacity):
        scores = scores + jnp.sum(
            jnp.where(owner_hit & (flat_rank[:, None] == r), mine[:, r][None, :], 0.0), axis=1
        )
    scores = scores.reshape(queries, candidates)
    _, divergence = distill(scores, teacher)

    query_part, passage_part = pair_grads(
        exponent_terms, exponent_total, recv_mask, recv_weight, recv_emb, passage_rows
    )
    passage_grad = jnp.einsum(
        "sp,sjd->jpd",
        passage_pick.astype(jnp.bfloat16),
        passage_part,
        preferred_element_type=jnp.float32,
    )
    returned_grads = lax.all_to_all(
        query_part.reshape(devices, capacity * query_len, width),
        AXES,
        split_axis=0,
        concat_axis=0,
        tiled=True,
    ).reshape(slots, query_len, width)
    query_grad = jnp.einsum(
        "sq,sid->qid",
        query_pick.astype(jnp.bfloat16),
        returned_grads,
        preferred_element_type=jnp.float32,
    )

    query_pre_grad = grad_pre_of(query_unit, query_norm, query_grad.reshape(queries * query_len, width))
    passage_pre_grad = grad_pre_of(
        passage_unit, passage_norm, passage_grad.reshape(passage_len * passages, width)
    )
    contract = (((0,), (0,)), ((), ()))
    local_grad = lax.dot_general(
        query_flat, query_pre_grad, contract, preferred_element_type=jnp.float32
    ) + lax.dot_general(passage_flat, passage_pre_grad, contract, preferred_element_type=jnp.float32)
    flat = jnp.concatenate([local_grad.reshape(-1), jnp.sum(divergence)[None]])
    total = all_sum(flat, devices)
    head_grad = total[: hidden * width].reshape(hidden, width)
    loss = total[hidden * width] / (queries * devices)
    return (scores, loss, head_grad)


def solution(mesh):
    return jax.shard_map(
        on_device,
        mesh=mesh,
        in_specs=(
            P(AXES, None, None),
            P(AXES, None, None),
            P(),
            P(AXES, None),
            P(AXES, None),
            P(AXES, None),
            P(AXES),
            P(AXES),
        ),
        out_specs=(P(AXES, None), P(), P()),
        check_vma=False,
    )
```
